32 devices in a mesh: req: 8 (over y, x, core), tp: 4 (over z).
Axes of the slice: x: 2, y: 2, z: 4, core: 2. Of those that a mesh axis runs over, the one named last changes fastest.
Arguments:
- final_states: float32 [16384, 1024], P('req'), may hold values from -50 to 50
- norm_gain: float32 [1024], replicated, may hold values from 0.1 to 1.9
- embedding: bfloat16 [32768, 1024], P('tp'), may hold values from -2 to 2
- targets: int32 [16384], P('req'), may hold values from 0 to 32767
- deal: int32 [8192], P('req'), may hold values from 0 to 16383, as said below
Outputs:
- logprob: float32 [16384], P('req')
- entropy: float32 [16384], P('req')
The draws below stay inside these ranges and needn't reach their ends.
Inputs may be any that keep to these rules, and one draw needn't show every extreme that they name: Every owned row is named at most once. The rows named of each owner device are a prefix of its 2048 rows (its sequence's live tokens), between 128 and 2048 rows long, and some owner device is named in full; the rest is padding. Each owner's live rows are dealt over all req devices, its own device included. Along each device's 8192 // 8 positions, in order, the owner device number deal // 2048 never decreases. At most 256 positions of one device name rows of one owner device, and some device reaches 256.
All inputs are finite; a program needn't handle non-finite values.
Results may differ from the reference program's by a relative error of at most 0.0031.
Values sent between devices are 32-bit elements; how exact they have to be, the bound alone decides.
No kernel may reach another device: no remote copies, remote signals or barrier semaphores. Data moves between devices by JAX's collectives and lax.ppermute only.
A program may use at most 128 MiB of HBM per device.

```python
import math
import jax
import jax.numpy as jnp
import numpy as np
from jax import lax

D = 1024
VOCAB = 32768
TOK_DEV = 1024
OWN_DEV = 2048
TOKENS = 8192
OWNED = 16384


def shared_direction(key):
    base = jax.random.normal(jax.random.fold_in(key, 5153), (1, D), jnp.float32)
    return jnp.clip(base, -3.0, 3.0)


def draw_final_states(key, part):
    keys = jax.random.split(jax.random.fold_in(key, 11), 3)
    row_scale = jnp.exp(jax.random.uniform(keys[0], (OWNED, 1), jnp.float32, 0.0, math.log(10.0)))
    common = shared_direction(key)
    lean = jax.random.uniform(keys[1], (OWNED, 1), jnp.float32, -2.0, 2.0)
    base = jnp.clip(jax.random.normal(keys[2], (OWNED, D), jnp.float32), -4.0, 4.0)
    mixed = (base + lean * common) / jnp.sqrt(1.0 + lean * lean)
    return row_scale * mixed


def draw_embedding(key, part):
    keys = jax.random.split(jax.random.fold_in(key, 23), 4)
    row_scale = jnp.exp(jax.random.uniform(keys[0], (VOCAB, 1), jnp.float32, math.log(0.3), math.log(3.0)))
    sign = jnp.where(jax.random.uniform(keys[2], (VOCAB, 1), jnp.float32) < 0.5, -1.0, 1.0)
    reach = jax.random.uniform(keys[3], (VOCAB, 1), jnp.float32, 4.0, 16.0)
    lift = jnp.where(row_scale < 1.8, sign * reach / D, 0.0) * shared_direction(key)
    base = jnp.clip(jax.random.normal(keys[1], (VOCAB, D), jnp.float32), -4.0, 4.0) * 0.06 * row_scale + lift
    return base.astype(jnp.bfloat16)


def draw_deal(key, part):
    owners = TOKENS // TOK_DEV
    keys = jax.random.split(jax.random.fold_in(key, 31), 4)
    margin = OWN_DEV // 16
    half_rows = OWN_DEV // 2
    first_len = jax.random.randint(keys[0], (1,), margin, half_rows - margin + 1, jnp.int32)
    second_len = jax.random.randint(keys[1], (1,), margin, half_rows - margin + 1, jnp.int32)
    pair_count = (owners - 4) // 2
    offsets = jax.random.randint(keys[2], (pair_count,), -(half_rows - margin), half_rows - margin + 1, jnp.int32)
    full_len = jnp.full((1,), OWN_DEV, jnp.int32)
    lengths = jnp.concatenate([full_len, first_len, second_len, OWN_DEV - first_len - second_len, half_rows + offsets, half_rows - offsets])
    lengths = lengths[jax.random.permutation(keys[3], owners)]
    live_rows = (jnp.arange(OWN_DEV, dtype=jnp.int32)[None, :] < lengths[:, None]).reshape(-1).astype(jnp.int32)
    order = jnp.cumsum(live_rows) - 1
    position = order % owners * TOK_DEV + order // owners
    position = jnp.where(live_rows == 1, position, TOKENS)
    return jnp.zeros((TOKENS,), jnp.int32).at[position].set(jnp.arange(OWNED, dtype=jnp.int32), mode='drop')


def with_ends(entries, stream_key, least, largest):
    index_at = [jax.random.randint(jax.random.fold_in(stream_key, axis), (), 0, length) for axis, length in enumerate(entries.shape)]
    longest = entries.shape.index(max(entries.shape))
    next_to = index_at[:longest] + [(index_at[longest] + 1) % entries.shape[longest]] + index_at[longest + 1:]
    return entries.at[tuple(index_at)].set(least).at[tuple(next_to)].set(largest)


def cumulative_ranks(number_of, skew):
    portions = [(1 << 20) // math.isqrt(standing ** skew) + 1 for standing in range(1, number_of + 1)]
    width = 1 + sum(portions) // (1 << 30)
    return np.cumsum(np.array([max(1, weight // width) for weight in portions]))


def skewed_ids(rng, dims, number_of, skew):
    grid = cumulative_ranks(number_of, skew)
    lot = jax.random.randint(jax.random.fold_in(rng, 1), dims, 0, int(grid[number_of - 1]))
    grade = jnp.searchsorted(jnp.asarray(grid, jnp.int32), lot, side="right")
    return jax.random.permutation(jax.random.fold_in(rng, 2), number_of)[grade].astype(jnp.int32)


def setup_inputs(seed: int = 0) -> dict:
    key_list = jax.random.split(jax.random.key(seed), 6)
    return {
        "final_states": draw_final_states(jax.random.fold_in(key_list[5], 71), 0),
        "norm_gain": jnp.clip(1.0 + 0.18 * jax.random.normal(key_list[1], (D,), jnp.float32), 0.1, 1.9),
        "embedding": draw_embedding(jax.random.fold_in(key_list[5], 71), 0),
        "targets": with_ends(skewed_ids(key_list[3], (OWNED,), VOCAB, 2), jax.random.fold_in(key_list[3], 3), 0, VOCAB - 1).astype(jnp.int32),
        "deal": draw_deal(jax.random.fold_in(key_list[5], 71), 0),
    }


def reference(final_states, norm_gain, embedding, targets, deal):
    if TOKENS % 512 == 0:
        block_rows = 512
    else:
        block_rows = TOKENS
    num_blocks = TOKENS // block_rows
    scored = final_states[deal]
    target_ids = targets[deal]
    table = embedding.astype(jnp.float32)

    def score_block(pieces):
        states, block_ids = pieces
        mean_square = lax.optimization_barrier(jnp.mean(states * states, axis=1, keepdims=True))
        normed = (states * lax.rsqrt(mean_square + 1e-06) * norm_gain[None, :]).astype(jnp.bfloat16)
        logits = lax.dot_general(normed.astype(jnp.float32), table, (((1,), (1,)), ((), ())), precision=lax.Precision.HIGHEST, preferred_element_type=jnp.float32)
        row_peak = lax.optimization_barrier(jnp.max(logits, axis=1))
        weights = jnp.exp(logits - row_peak[:, None])
        exp_total = lax.optimization_barrier(jnp.sum(weights, axis=1))
        moment = lax.optimization_barrier(jnp.sum(weights * logits, axis=1))
        log_total = row_peak + jnp.log(exp_total)
        chosen = jnp.take_along_axis(logits, block_ids[:, None], axis=1)[:, 0]
        return (chosen - log_total, log_total - moment / exp_total)
    logprob_rows, entropy_rows = lax.map(score_block, (scored.reshape(num_blocks, block_rows, D), target_ids.reshape(num_blocks, block_rows)))
    logprob = jnp.zeros((OWNED,), jnp.float32).at[deal].set(logprob_rows.reshape(-1))
    entropy = jnp.zeros((OWNED,), jnp.float32).at[deal].set(entropy_rows.reshape(-1))
    return (logprob, entropy)
```

```python
import jax
import jax.numpy as jnp
from jax import lax
from jax.sharding import PartitionSpec as P


def rms_normed(states, norm_gain):
    mean_square = jnp.mean(states * states, axis=1, keepdims=True)
    return (states * lax.rsqrt(mean_square + 1e-06) * norm_gain[None, :]).astype(jnp.bfloat16)


def shard_stats(normed, embedding, in_shard_id):
    logits = lax.dot_general(
        normed, embedding, (((1,), (1,)), ((), ())), preferred_element_type=jnp.float32
    )
    peak = jnp.max(logits, axis=1)
    weights = jnp.exp(logits - peak[:, None])
    total = jnp.sum(weights, axis=1)
    moment = jnp.sum(weights * logits, axis=1)
    cols = lax.broadcasted_iota(jnp.int32, logits.shape, 1)
    chosen = jnp.sum(jnp.where(cols == in_shard_id[:, None], logits, 0.0), axis=1)
    return jnp.stack((peak, total, moment, chosen))


def body(final_states, norm_gain, embedding, targets, deal):
    owners = lax.axis_size("req")
    own_rows = final_states.shape[0]
    shard_cols = embedding.shape[0]
    vocab_start = lax.axis_index("tp") * shard_cols
    member = (deal[:, None] // own_rows == jnp.arange(owners, dtype=jnp.int32)[None, :])
    counts = lax.psum(jnp.sum(member.astype(jnp.int32), axis=0), "req")
    live_count = counts[lax.axis_index("req")]
    live = jnp.arange(own_rows, dtype=jnp.int32) < live_count

    in_shard_id = targets - vocab_start
    block = 512 if own_rows % 512 == 0 else own_rows
    parts = []
    for b in range(own_rows // block):
        rows = slice(b * block, (b + 1) * block)
        normed = rms_normed(final_states[rows], norm_gain)
        parts.append(shard_stats(normed, embedding, in_shard_id[rows]))
    stats = jnp.concatenate(parts, axis=1)
    gathered = lax.all_gather(stats, "tp")
    peaks = gathered[:, 0]
    row_peak = jnp.max(peaks, axis=0)
    scale = jnp.exp(peaks - row_peak[None, :])
    exp_total = jnp.sum(gathered[:, 1] * scale, axis=0)
    moment = jnp.sum(gathered[:, 2] * scale, axis=0)
    chosen = jnp.sum(gathered[:, 3], axis=0)
    log_total = row_peak + jnp.log(exp_total)
    expected = moment / exp_total
    logprob = jnp.where(live, chosen - log_total, 0.0)
    entropy = jnp.where(live, log_total - expected, 0.0)
    return (logprob, entropy)


def solution(mesh):
    return jax.shard_map(
        body,
        mesh=mesh,
        in_specs=(P("req", None), P(), P("tp", None), P("req"), P("req")),
        out_specs=(P("req"), P("req")),
        check_vma=False,
    )
```

```python
import functools

import jax
import jax.numpy as jnp
from jax import lax
from jax.experimental import pallas as pl
from jax.experimental.pallas import tpu as pltpu
from jax.sharding import PartitionSpec as P


def rms_normed(states, norm_gain):
    mean_square = jnp.mean(states * states, axis=1, keepdims=True)
    return (states * lax.rsqrt(mean_square + 1e-06) * norm_gain[None, :]).astype(jnp.bfloat16)


def shard_stats_xla(normed, embedding, in_shard_id):
    logits = lax.dot_general(
        normed, embedding, (((1,), (1,)), ((), ())), preferred_element_type=jnp.float32
    )
    peak = jnp.max(logits, axis=1)
    weights = jnp.exp(logits - peak[:, None])
    total = jnp.sum(weights, axis=1)
    moment = jnp.sum(weights * logits, axis=1)
    cols = lax.broadcasted_iota(jnp.int32, logits.shape, 1)
    chosen = jnp.sum(jnp.where(cols == in_shard_id[:, None], logits, 0.0), axis=1)
    return jnp.stack((peak, total, moment, chosen))


def stats_kernel(row_block, normed_ref, emb_ref, ids_ref, peak_ref, total_ref, moment_ref, chosen_ref):
    j = pl.program_id(0)
    col_block = emb_ref.shape[0]

    @pl.when(j == 0)
    def _():
        peak_ref[...] = jnp.full(peak_ref.shape, -1e30, jnp.float32)
        total_ref[...] = jnp.zeros(total_ref.shape, jnp.float32)
        moment_ref[...] = jnp.zeros(moment_ref.shape, jnp.float32)
        chosen_ref[...] = jnp.zeros(chosen_ref.shape, jnp.float32)

    table = emb_ref[...]
    cols = lax.broadcasted_iota(jnp.int32, (row_block, col_block), 1)

    def chunk(r, carry):
        rows = pl.ds(pl.multiple_of(r * row_block, row_block), row_block)
        logits = lax.dot_general(
            normed_ref[rows, :], table, (((1,), (1,)), ((), ())),
            preferred_element_type=jnp.float32,
        )
        old_peak = peak_ref[rows, :]
        new_peak = jnp.maximum(old_peak, jnp.max(logits, axis=1, keepdims=True))
        weights = jnp.exp(logits - new_peak)
        scale = jnp.exp(old_peak - new_peak)
        total_ref[rows, :] = total_ref[rows, :] * scale + jnp.sum(weights, axis=1, keepdims=True)
        moment_ref[rows, :] = moment_ref[rows, :] * scale + jnp.sum(
            weights * logits, axis=1, keepdims=True
        )
        peak_ref[rows, :] = new_peak
        local_id = ids_ref[rows, :] - j * col_block
        chosen_ref[rows, :] = chosen_ref[rows, :] + jnp.sum(
            jnp.where(cols == local_id, logits, 0.0), axis=1, keepdims=True
        )
        return carry

    lax.fori_loop(0, normed_ref.shape[0] // row_block, chunk, 0)


def shard_stats(normed, embedding, in_shard_id, col_block=1024, row_block=256):
    rows, width = normed.shape
    vocab = embedding.shape[0]
    col_block = min(col_block, vocab)
    row_block = min(row_block, rows)
    stat = jax.ShapeDtypeStruct((rows, 1), jnp.float32)
    resident = pl.BlockSpec((rows, 1), lambda j: (0, 0))
    outs = pl.pallas_call(
        functools.partial(stats_kernel, row_block),
        grid=(vocab // col_block,),
        in_specs=[
            pl.BlockSpec((rows, width), lambda j: (0, 0)),
            pl.BlockSpec((col_block, width), lambda j: (j, 0)),
            pl.BlockSpec((rows, 1), lambda j: (0, 0)),
        ],
        out_specs=[resident] * 4,
        out_shape=[stat] * 4,
        compiler_params=pltpu.CompilerParams(
            dimension_semantics=("arbitrary",), vmem_limit_bytes=48 * 1024 * 1024
        ),
        cost_estimate=pl.CostEstimate(
            flops=2 * rows * vocab * width,
            transcendentals=rows * vocab,
            bytes_accessed=rows * width * 2 + vocab * width * 2 + rows * 20,
        ),
    )(normed, embedding, in_shard_id[:, None])
    return jnp.stack([o[:, 0] for o in outs])


def body(final_states, norm_gain, embedding, targets, deal):
    owners = lax.axis_size("req")
    own_rows = final_states.shape[0]
    shard_cols = embedding.shape[0]
    vocab_start = lax.axis_index("tp") * shard_cols
    member = (deal[:, None] // own_rows == jnp.arange(owners, dtype=jnp.int32)[None, :])
    counts = lax.all_gather(jnp.sum(member.astype(jnp.int32), axis=0), "req")
    live_count = jnp.sum(counts[:, lax.axis_index("req")])
    live = jnp.arange(own_rows, dtype=jnp.int32) < live_count

    normed = rms_normed(final_states, norm_gain)
    stats = shard_stats(normed, embedding, targets - vocab_start)
    gathered = lax.all_gather(stats, "tp")
    peaks = gathered[:, 0]
    row_peak = jnp.max(peaks, axis=0)
    scale = jnp.exp(peaks - row_peak[None, :])
    exp_total = jnp.sum(gathered[:, 1] * scale, axis=0)
    moment = jnp.sum(gathered[:, 2] * scale, axis=0)
    chosen = jnp.sum(gathered[:, 3], axis=0)
    log_total = row_peak + jnp.log(exp_total)
    expected = moment / exp_total
    logprob = jnp.where(live, chosen - log_total, 0.0)
    entropy = jnp.where(live, log_total - expected, 0.0)
    return (logprob, entropy)


def solution(mesh):
    return jax.shard_map(
        body,
        mesh=mesh,
        in_specs=(P("req", None), P(), P("tp", None), P("req"), P("req")),
        out_specs=(P("req"), P("req")),
        check_vma=False,
    )
```

```python
import functools

import jax
import jax.numpy as jnp
from jax import lax
from jax.experimental import pallas as pl
from jax.experimental.pallas import tpu as pltpu
from jax.sharding import PartitionSpec as P


def rms_normed(states, norm_gain):
    mean_square = jnp.mean(states * states, axis=1, keepdims=True)
    return (states * lax.rsqrt(mean_square + 1e-06) * norm_gain[None, :]).astype(jnp.bfloat16)


def shard_stats_xla(normed, embedding, in_shard_id):
    logits = lax.dot_general(
        normed, embedding, (((1,), (1,)), ((), ())), preferred_element_type=jnp.float32
    )
    peak = jnp.max(logits, axis=1)
    weights = jnp.exp(logits - peak[:, None])
    total = jnp.sum(weights, axis=1)
    moment = jnp.sum(weights * logits, axis=1)
    cols = lax.broadcasted_iota(jnp.int32, logits.shape, 1)
    chosen = jnp.sum(jnp.where(cols == in_shard_id[:, None], logits, 0.0), axis=1)
    return jnp.stack((peak, total, moment, chosen))


def stats_kernel(row_block, normed_ref, emb_ref, ids_ref, peak_ref, total_ref, moment_ref, chosen_ref):
    j = pl.program_id(0)
    col_block = emb_ref.shape[0]

    @pl.when(j == 0)
    def _():
        peak_ref[...] = jnp.full(peak_ref.shape, -1e30, jnp.float32)
        total_ref[...] = jnp.zeros(total_ref.shape, jnp.float32)
        moment_ref[...] = jnp.zeros(moment_ref.shape, jnp.float32)
        chosen_ref[...] = jnp.zeros(chosen_ref.shape, jnp.float32)

    table = emb_ref[...]
    vocab_ids = lax.broadcasted_iota(jnp.int32, (col_block, row_block), 0)

    def chunk(r, carry):
        start = pl.multiple_of(r * row_block, row_block)
        rows = pl.ds(start, row_block)
        logits = lax.dot_general(
            table, normed_ref[rows, :], (((1,), (1,)), ((), ())),
            preferred_element_type=jnp.float32,
        )
        old_peak = peak_ref[:, rows]
        new_peak = jnp.maximum(old_peak, jnp.max(logits, axis=0, keepdims=True))
        weights = jnp.exp(logits - new_peak)
        scale = jnp.exp(old_peak - new_peak)
        total_ref[:, rows] = total_ref[:, rows] * scale + jnp.sum(weights, axis=0, keepdims=True)
        moment_ref[:, rows] = moment_ref[:, rows] * scale + jnp.sum(
            weights * logits, axis=0, keepdims=True
        )
        peak_ref[:, rows] = new_peak
        local_id = ids_ref[:, rows] - j * col_block
        chosen_ref[:, rows] = chosen_ref[:, rows] + jnp.sum(
            jnp.where(vocab_ids == local_id, logits, 0.0), axis=0, keepdims=True
        )
        return carry

    lax.fori_loop(0, normed_ref.shape[0] // row_block, chunk, 0)


def shard_stats(normed, embedding, in_shard_id, col_block=1024, row_block=256):
    rows, width = normed.shape
    vocab = embedding.shape[0]
    col_block = min(col_block, vocab)
    row_block = min(row_block, rows)
    stat = jax.ShapeDtypeStruct((1, rows), jnp.float32)
    resident = pl.BlockSpec((1, rows), lambda j: (0, 0))
    outs = pl.pallas_call(
        functools.partial(stats_kernel, row_block),
        grid=(vocab // col_block,),
        in_specs=[
            pl.BlockSpec((rows, width), lambda j: (0, 0)),
            pl.BlockSpec((col_block, width), lambda j: (j, 0)),
            pl.BlockSpec((1, rows), lambda j: (0, 0)),
        ],
        out_specs=[resident] * 4,
        out_shape=[stat] * 4,
        compiler_params=pltpu.CompilerParams(
            dimension_semantics=("arbitrary",), vmem_limit_bytes=48 * 1024 * 1024
        ),
        cost_estimate=pl.CostEstimate(
            flops=2 * rows * vocab * width,
            transcendentals=rows * vocab,
            bytes_accessed=rows * width * 2 + vocab * width * 2 + rows * 20,
        ),
    )(normed, embedding, in_shard_id[None, :])
    return jnp.concatenate(outs, axis=0)


def body(final_states, norm_gain, embedding, targets, deal):
    owners = lax.axis_size("req")
    own_rows = final_states.shape[0]
    shard_cols = embedding.shape[0]
    vocab_start = lax.axis_index("tp") * shard_cols
    member = (deal[:, None] // own_rows == jnp.arange(owners, dtype=jnp.int32)[None, :])
    counts = lax.all_gather(jnp.sum(member.astype(jnp.int32), axis=0), "req")
    live_count = jnp.sum(counts[:, lax.axis_index("req")])
    live = jnp.arange(own_rows, dtype=jnp.int32) < live_count

    normed = rms_normed(final_states, norm_gain)
    stats = shard_stats(normed, embedding, targets - vocab_start)
    gathered = lax.all_gather(stats, "tp")
    peaks = gathered[:, 0]
    row_peak = jnp.max(peaks, axis=0)
    scale = jnp.exp(peaks - row_peak[None, :])
    exp_total = jnp.sum(gathered[:, 1] * scale, axis=0)
    moment = jnp.sum(gathered[:, 2] * scale, axis=0)
    chosen = jnp.sum(gathered[:, 3], axis=0)
    log_total = row_peak + jnp.log(exp_total)
    expected = moment / exp_total
    logprob = jnp.where(live, chosen - log_total, 0.0)
    entropy = jnp.where(live, log_total - expected, 0.0)
    return (logprob, entropy)


def solution(mesh):
    return jax.shard_map(
        body,
        mesh=mesh,
        in_specs=(P("req", None), P(), P("tp", None), P("req"), P("req")),
        out_specs=(P("req"), P("req")),
        check_vma=False,
    )
```

```python
import functools

import jax
import jax.numpy as jnp
from jax import lax
from jax.experimental import pallas as pl
from jax.experimental.pallas import tpu as pltpu
from jax.sharding import PartitionSpec as P


def rms_normed(states, norm_gain):
    mean_square = jnp.mean(states * states, axis=1, keepdims=True)
    return (states * lax.rsqrt(mean_square + 1e-06) * norm_gain[None, :]).astype(jnp.bfloat16)


def shard_stats_xla(normed, embedding, in_shard_id):
    logits = lax.dot_general(
        normed, embedding, (((1,), (1,)), ((), ())), preferred_element_type=jnp.float32
    )
    peak = jnp.max(logits, axis=1)
    weights = jnp.exp(logits - peak[:, None])
    total = jnp.sum(weights, axis=1)
    moment = jnp.sum(weights * logits, axis=1)
    cols = lax.broadcasted_iota(jnp.int32, logits.shape, 1)
    chosen = jnp.sum(jnp.where(cols == in_shard_id[:, None], logits, 0.0), axis=1)
    return jnp.stack((peak, total, moment, chosen))


def stats_kernel(row_block, normed_ref, emb_ref, ids_ref, peak_ref, total_ref, moment_ref, chosen_ref):
    j = pl.program_id(0)
    col_block = emb_ref.shape[0]

    @pl.when(j == 0)
    def _():
        peak_ref[...] = jnp.full(peak_ref.shape, -1e30, jnp.float32)
        total_ref[...] = jnp.zeros(total_ref.shape, jnp.float32)
        moment_ref[...] = jnp.zeros(moment_ref.shape, jnp.float32)
        chosen_ref[...] = jnp.zeros(chosen_ref.shape, jnp.float32)

    table = emb_ref[...]
    vocab_ids = lax.broadcasted_iota(jnp.int32, (col_block, row_block), 0)

    def chunk(r, carry):
        start = pl.multiple_of(r * row_block, row_block)
        rows = pl.ds(start, row_block)
        logits = lax.dot_general(
            table, normed_ref[rows, :], (((1,), (1,)), ((), ())),
            preferred_element_type=jnp.float32,
        )
        old_peak = peak_ref[:, rows]
        new_peak = jnp.maximum(old_peak, jnp.max(logits, axis=0, keepdims=True))
        weights = jnp.exp(logits - new_peak)
        scale = jnp.exp(old_peak - new_peak)
        total_ref[:, rows] = total_ref[:, rows] * scale + jnp.sum(weights, axis=0, keepdims=True)
        moment_ref[:, rows] = moment_ref[:, rows] * scale + jnp.sum(
            weights * logits, axis=0, keepdims=True
        )
        peak_ref[:, rows] = new_peak
        local_id = ids_ref[:, rows] - j * col_block
        chosen_ref[:, rows] = chosen_ref[:, rows] + jnp.sum(
            jnp.where(vocab_ids == local_id, logits, 0.0), axis=0, keepdims=True
        )
        return carry

    lax.fori_loop(0, normed_ref.shape[0] // row_block, chunk, 0)


def shard_stats(normed, embedding, in_shard_id, col_block=1024, row_block=256):
    rows, width = normed.shape
    vocab = embedding.shape[0]
    col_block = min(col_block, vocab)
    row_block = min(row_block, rows)
    stat = jax.ShapeDtypeStruct((1, rows), jnp.float32)
    resident = pl.BlockSpec((1, rows), lambda j: (0, 0))
    outs = pl.pallas_call(
        functools.partial(stats_kernel, row_block),
        grid=(vocab // col_block,),
        in_specs=[
            pl.BlockSpec((rows, width), lambda j: (0, 0)),
            pl.BlockSpec((col_block, width), lambda j: (j, 0)),
            pl.BlockSpec((1, rows), lambda j: (0, 0)),
        ],
        out_specs=[resident] * 4,
        out_shape=[stat] * 4,
        compiler_params=pltpu.CompilerParams(
            dimension_semantics=("arbitrary",), vmem_limit_bytes=48 * 1024 * 1024
        ),
        cost_estimate=pl.CostEstimate(
            flops=2 * rows * vocab * width,
            transcendentals=rows * vocab,
            bytes_accessed=rows * width * 2 + vocab * width * 2 + rows * 20,
        ),
    )(normed, embedding, in_shard_id[None, :])
    return jnp.concatenate(outs, axis=0)


def combine_over_tp(stats):
    group = lax.axis_size("tp")
    me = lax.axis_index("tp")
    pieces = [stats]
    for shift in range(1, group):
        pieces.append(
            lax.ppermute(stats, "tp", [(d, (d + shift) % group) for d in range(group)])
        )
    gathered = jnp.stack(pieces)
    peaks = gathered[:, 0]
    row_peak = jnp.max(peaks, axis=0)
    scale = jnp.exp(peaks - row_peak[None, :])
    exp_total = jnp.sum(gathered[:, 1] * scale, axis=0)
    moment = jnp.sum(gathered[:, 2] * scale, axis=0)
    chosen = jnp.sum(gathered[:, 3], axis=0)
    log_total = row_peak + jnp.log(exp_total)
    expected = moment / exp_total
    return chosen - log_total, log_total - expected


def live_count_of_owner(deal, own_rows):
    owners = lax.axis_size("req")
    me = lax.axis_index("req")
    member = (deal[:, None] // own_rows == jnp.arange(owners, dtype=jnp.int32)[None, :])
    counts = jnp.sum(member.astype(jnp.int32), axis=0)
    received = [lax.dynamic_slice(counts, (me,), (1,))]
    for shift in range(1, owners):
        sent = lax.dynamic_slice(counts, ((me + shift) % owners,), (1,))
        received.append(
            lax.ppermute(sent, "req", [(d, (d + shift) % owners) for d in range(owners)])
        )
    return jnp.sum(jnp.concatenate(received))


def body(final_states, norm_gain, embedding, targets, deal):
    own_rows = final_states.shape[0]
    shard_cols = embedding.shape[0]
    vocab_start = lax.axis_index("tp") * shard_cols
    live_count = live_count_of_owner(deal, own_rows)

    normed = rms_normed(final_states, norm_gain)
    in_shard_id = targets - vocab_start
    half = own_rows // 2 if own_rows % 512 == 0 else own_rows
    logprob_parts, entropy_parts = [], []
    for start in range(0, own_rows, half):
        rows_normed = normed[start:start + half]
        if start > 0:
            rows_normed, live_count = lax.optimization_barrier((rows_normed, live_count))
        stats = shard_stats(rows_normed, embedding, in_shard_id[start:start + half])
        logprob_part, entropy_part = combine_over_tp(stats)
        logprob_parts.append(logprob_part)
        entropy_parts.append(entropy_part)
    live = jnp.arange(own_rows, dtype=jnp.int32) < live_count
    logprob = jnp.where(live, jnp.concatenate(logprob_parts), 0.0)
    entropy = jnp.where(live, jnp.concatenate(entropy_parts), 0.0)
    return (logprob, entropy)


def solution(mesh):
    return jax.shard_map(
        body,
        mesh=mesh,
        in_specs=(P("req", None), P(), P("tp", None), P("req"), P("req")),
        out_specs=(P("req"), P("req")),
        check_vma=False,
    )
```

```python
import functools

import jax
import jax.numpy as jnp
from jax import lax
from jax.experimental import pallas as pl
from jax.experimental.pallas import tpu as pltpu
from jax.sharding import PartitionSpec as P


def rms_normed(states, norm_gain):
    mean_square = jnp.mean(states * states, axis=1, keepdims=True)
    return (states * lax.rsqrt(mean_square + 1e-06) * norm_gain[None, :]).astype(jnp.bfloat16)


def shard_stats_xla(normed, embedding, in_shard_id):
    logits = lax.dot_general(
        normed, embedding, (((1,), (1,)), ((), ())), preferred_element_type=jnp.float32
    )
    peak = jnp.max(logits, axis=1)
    weights = jnp.exp(logits - peak[:, None])
    total = jnp.sum(weights, axis=1)
    moment = jnp.sum(weights * logits, axis=1)
    cols = lax.broadcasted_iota(jnp.int32, logits.shape, 1)
    chosen = jnp.sum(jnp.where(cols == in_shard_id[:, None], logits, 0.0), axis=1)
    return jnp.stack((peak, total, moment, chosen))


def stats_kernel(row_block, normed_ref, emb_ref, ids_ref, peak_ref, total_ref, moment_ref, chosen_ref):
    j = pl.program_id(0)
    col_block = emb_ref.shape[0]

    @pl.when(j == 0)
    def _():
        peak_ref[...] = jnp.full(peak_ref.shape, -1e30, jnp.float32)
        total_ref[...] = jnp.zeros(total_ref.shape, jnp.float32)
        moment_ref[...] = jnp.zeros(moment_ref.shape, jnp.float32)
        chosen_ref[...] = jnp.zeros(chosen_ref.shape, jnp.float32)

    table = emb_ref[...]
    vocab_ids = lax.broadcasted_iota(jnp.int32, (col_block, row_block), 0)

    def chunk(r, carry):
        start = pl.multiple_of(r * row_block, row_block)
        rows = pl.ds(start, row_block)
        logits = lax.dot_general(
            table, normed_ref[rows, :], (((1,), (1,)), ((), ())),
            preferred_element_type=jnp.float32,
        )
        old_peak = peak_ref[:, rows]
        new_peak = jnp.maximum(old_peak, jnp.max(logits, axis=0, keepdims=True))
        weights = jnp.exp(logits - new_peak)
        scale = jnp.exp(old_peak - new_peak)
        total_ref[:, rows] = total_ref[:, rows] * scale + jnp.sum(weights, axis=0, keepdims=True)
        moment_ref[:, rows] = moment_ref[:, rows] * scale + jnp.sum(
            weights * logits, axis=0, keepdims=True
        )
        peak_ref[:, rows] = new_peak
        local_id = ids_ref[:, rows] - j * col_block
        chosen_ref[:, rows] = chosen_ref[:, rows] + jnp.sum(
            jnp.where(vocab_ids == local_id, logits, 0.0), axis=0, keepdims=True
        )
        return carry

    lax.fori_loop(0, normed_ref.shape[0] // row_block, chunk, 0, unroll=True)


def shard_stats(normed, embedding, in_shard_id, col_block=1024, row_block=256):
    rows, width = normed.shape
    vocab = embedding.shape[0]
    col_block = min(col_block, vocab)
    row_block = min(row_block, rows)
    stat = jax.ShapeDtypeStruct((1, rows), jnp.float32)
    resident = pl.BlockSpec((1, rows), lambda j: (0, 0))
    outs = pl.pallas_call(
        functools.partial(stats_kernel, row_block),
        grid=(vocab // col_block,),
        in_specs=[
            pl.BlockSpec((rows, width), lambda j: (0, 0)),
            pl.BlockSpec((col_block, width), lambda j: (j, 0)),
            pl.BlockSpec((1, rows), lambda j: (0, 0)),
        ],
        out_specs=[resident] * 4,
        out_shape=[stat] * 4,
        compiler_params=pltpu.CompilerParams(
            dimension_semantics=("arbitrary",), vmem_limit_bytes=48 * 1024 * 1024
        ),
        cost_estimate=pl.CostEstimate(
            flops=2 * rows * vocab * width,
            transcendentals=rows * vocab,
            bytes_accessed=rows * width * 2 + vocab * width * 2 + rows * 20,
        ),
    )(normed, embedding, in_shard_id[None, :])
    return jnp.concatenate(outs, axis=0)


def body(final_states, norm_gain, embedding, targets, deal):
    owners = lax.axis_size("req")
    own_rows = final_states.shape[0]
    shard_cols = embedding.shape[0]
    vocab_start = lax.axis_index("tp") * shard_cols
    member = (deal[:, None] // own_rows == jnp.arange(owners, dtype=jnp.int32)[None, :])
    counts = lax.all_gather(jnp.sum(member.astype(jnp.int32), axis=0), "req")
    live_count = jnp.sum(counts[:, lax.axis_index("req")])
    live = jnp.arange(own_rows, dtype=jnp.int32) < live_count

    normed = rms_normed(final_states, norm_gain)
    stats = shard_stats(normed, embedding, targets - vocab_start)
    gathered = lax.all_gather(stats, "tp")
    peaks = gathered[:, 0]
    row_peak = jnp.max(peaks, axis=0)
    scale = jnp.exp(peaks - row_peak[None, :])
    exp_total = jnp.sum(gathered[:, 1] * scale, axis=0)
    moment = jnp.sum(gathered[:, 2] * scale, axis=0)
    chosen = jnp.sum(gathered[:, 3], axis=0)
    log_total = row_peak + jnp.log(exp_total)
    expected = moment / exp_total
    logprob = jnp.where(live, chosen - log_total, 0.0)
    entropy = jnp.where(live, log_total - expected, 0.0)
    return (logprob, entropy)


def solution(mesh):
    return jax.shard_map(
        body,
        mesh=mesh,
        in_specs=(P("req", None), P(), P("tp", None), P("req"), P("req")),
        out_specs=(P("req"), P("req")),
        check_vma=False,
    )
```

```python
import functools

import jax
import jax.numpy as jnp
from jax import lax
from jax.experimental import pallas as pl
from jax.experimental.pallas import tpu as pltpu
from jax.sharding import PartitionSpec as P


def rms_normed(states, norm_gain):
    mean_square = jnp.mean(states * states, axis=1, keepdims=True)
    return (states * lax.rsqrt(mean_square + 1e-06) * norm_gain[None, :]).astype(jnp.bfloat16)


def shard_stats_xla(normed, embedding, in_shard_id):
    logits = lax.dot_general(
        normed, embedding, (((1,), (1,)), ((), ())), preferred_element_type=jnp.float32
    )
    peak = jnp.max(logits, axis=1)
    weights = jnp.exp(logits - peak[:, None])
    total = jnp.sum(weights, axis=1)
    moment = jnp.sum(weights * logits, axis=1)
    cols = lax.broadcasted_iota(jnp.int32, logits.shape, 1)
    chosen = jnp.sum(jnp.where(cols == in_shard_id[:, None], logits, 0.0), axis=1)
    return jnp.stack((peak, total, moment, chosen))


LIFT = 40.0
SAFE = 60.0


def stats_kernel(row_block, normed_ref, emb_ref, ids_ref, peak_ref, total_ref, moment_ref, chosen_ref, saved_ref):
    j = pl.program_id(0)
    col_block = emb_ref.shape[0]
    vocab_ids = lax.broadcasted_iota(jnp.int32, (col_block, row_block), 0)
    stats = (peak_ref, total_ref, moment_ref, chosen_ref)

    @pl.when(j == 0)
    def _():
        peak_ref[...] = jnp.full(peak_ref.shape, -1e30, jnp.float32)
        total_ref[...] = jnp.zeros(total_ref.shape, jnp.float32)
        moment_ref[...] = jnp.zeros(moment_ref.shape, jnp.float32)
        chosen_ref[...] = jnp.zeros(chosen_ref.shape, jnp.float32)

    def logits_of(rows):
        return lax.dot_general(
            emb_ref[...], normed_ref[rows, :], (((1,), (1,)), ((), ())),
            preferred_element_type=jnp.float32,
        )

    def add_chosen(rows, logits):
        local_id = ids_ref[:, rows] - j * col_block
        chosen_ref[:, rows] = chosen_ref[:, rows] + jnp.sum(
            jnp.where(vocab_ids == local_id, logits, 0.0), axis=0, keepdims=True
        )

    def rows_of(r):
        return pl.ds(pl.multiple_of(r * row_block, row_block), row_block)

    def exact_chunk(r, carry):
        rows = rows_of(r)
        logits = logits_of(rows)
        old_peak = peak_ref[:, rows]
        new_peak = jnp.maximum(old_peak, jnp.max(logits, axis=0, keepdims=True))
        weights = jnp.exp(logits - new_peak)
        scale = jnp.exp(old_peak - new_peak)
        total_ref[:, rows] = total_ref[:, rows] * scale + jnp.sum(weights, axis=0, keepdims=True)
        moment_ref[:, rows] = moment_ref[:, rows] * scale + jnp.sum(weights * logits, axis=0, keepdims=True)
        peak_ref[:, rows] = new_peak
        add_chosen(rows, logits)
        return carry

    def fast_chunk(r, worst):
        rows = rows_of(r)
        logits = logits_of(rows)
        old_peak = peak_ref[:, rows]
        shift = old_peak + LIFT
        tile_peak = jnp.max(logits, axis=0, keepdims=True)
        weights = jnp.exp(logits - shift)
        new_peak = jnp.maximum(old_peak, tile_peak)
        scale = jnp.exp(old_peak - new_peak)
        part_scale = jnp.exp(shift - new_peak)
        total_ref[:, rows] = total_ref[:, rows] * scale + jnp.sum(weights, axis=0, keepdims=True) * part_scale
        moment_ref[:, rows] = moment_ref[:, rows] * scale + jnp.sum(weights * logits, axis=0, keepdims=True) * part_scale
        peak_ref[:, rows] = new_peak
        add_chosen(rows, logits)
        return jnp.maximum(worst, tile_peak - old_peak)

    n_chunks = normed_ref.shape[0] // row_block

    @pl.when(j == 0)
    def _():
        lax.fori_loop(0, n_chunks, exact_chunk, 0, unroll=True)

    @pl.when(j > 0)
    def _():
        for k, ref in enumerate(stats):
            saved_ref[k:k + 1, :] = ref[...]
        worst = lax.fori_loop(
            0, n_chunks, fast_chunk, jnp.full((1, row_block), -1e30, jnp.float32), unroll=True
        )

        @pl.when(jnp.max(worst) > SAFE)
        def _():
            for k, ref in enumerate(stats):
                ref[...] = saved_ref[k:k + 1, :]
            lax.fori_loop(0, n_chunks, exact_chunk, 0, unroll=True)


def shard_stats(normed, embedding, in_shard_id, col_block=1024, row_block=256):
    rows, width = normed.shape
    vocab = embedding.shape[0]
    col_block = min(col_block, vocab)
    row_block = min(row_block, rows)
    stat = jax.ShapeDtypeStruct((1, rows), jnp.float32)
    resident = pl.BlockSpec((1, rows), lambda j: (0, 0))
    outs = pl.pallas_call(
        functools.partial(stats_kernel, row_block),
        grid=(vocab // col_block,),
        in_specs=[
            pl.BlockSpec((rows, width), lambda j: (0, 0)),
            pl.BlockSpec((col_block, width), lambda j: (j, 0)),
            pl.BlockSpec((1, rows), lambda j: (0, 0)),
        ],
        out_specs=[resident] * 4,
        out_shape=[stat] * 4,
        scratch_shapes=[pltpu.VMEM((4, rows), jnp.float32)],
        compiler_params=pltpu.CompilerParams(
            dimension_semantics=("arbitrary",), vmem_limit_bytes=48 * 1024 * 1024
        ),
        cost_estimate=pl.CostEstimate(
            flops=2 * rows * vocab * width,
            transcendentals=rows * vocab,
            bytes_accessed=rows * width * 2 + vocab * width * 2 + rows * 20,
        ),
    )(normed, embedding, in_shard_id[None, :])
    return jnp.concatenate(outs, axis=0)


def body(final_states, norm_gain, embedding, targets, deal):
    owners = lax.axis_size("req")
    own_rows = final_states.shape[0]
    shard_cols = embedding.shape[0]
    vocab_start = lax.axis_index("tp") * shard_cols
    member = (deal[:, None] // own_rows == jnp.arange(owners, dtype=jnp.int32)[None, :])
    counts = lax.all_gather(jnp.sum(member.astype(jnp.int32), axis=0), "req")
    live_count = jnp.sum(counts[:, lax.axis_index("req")])
    live = jnp.arange(own_rows, dtype=jnp.int32) < live_count

    normed = rms_normed(final_states, norm_gain)
    stats = shard_stats(normed, embedding, targets - vocab_start)
    gathered = lax.all_gather(stats, "tp")
    peaks = gathered[:, 0]
    row_peak = jnp.max(peaks, axis=0)
    scale = jnp.exp(peaks - row_peak[None, :])
    exp_total = jnp.sum(gathered[:, 1] * scale, axis=0)
    moment = jnp.sum(gathered[:, 2] * scale, axis=0)
    chosen = jnp.sum(gathered[:, 3], axis=0)
    log_total = row_peak + jnp.log(exp_total)
    expected = moment / exp_total
    logprob = jnp.where(live, chosen - log_total, 0.0)
    entropy = jnp.where(live, log_total - expected, 0.0)
    return (logprob, entropy)


def solution(mesh):
    return jax.shard_map(
        body,
        mesh=mesh,
        in_specs=(P("req", None), P(), P("tp", None), P("req"), P("req")),
        out_specs=(P("req"), P("req")),
        check_vma=False,
    )
```

```python
import functools

import jax
import jax.numpy as jnp
from jax import lax
from jax.experimental import pallas as pl
from jax.experimental.pallas import tpu as pltpu
from jax.sharding import PartitionSpec as P


def rms_normed(states, norm_gain):
    mean_square = jnp.mean(states * states, axis=1, keepdims=True)
    return (states * lax.rsqrt(mean_square + 1e-06) * norm_gain[None, :]).astype(jnp.bfloat16)


def shard_stats_xla(normed, embedding, in_shard_id):
    logits = lax.dot_general(
        normed, embedding, (((1,), (1,)), ((), ())), preferred_element_type=jnp.float32
    )
    peak = jnp.max(logits, axis=1)
    weights = jnp.exp(logits - peak[:, None])
    total = jnp.sum(weights, axis=1)
    moment = jnp.sum(weights * logits, axis=1)
    cols = lax.broadcasted_iota(jnp.int32, logits.shape, 1)
    chosen = jnp.sum(jnp.where(cols == in_shard_id[:, None], logits, 0.0), axis=1)
    return jnp.stack((peak, total, moment, chosen))


LIFT = 40.0
SAFE = 60.0


def stats_kernel(row_block, normed_ref, emb_ref, ids_ref, peak_ref, total_ref, moment_ref, chosen_ref, saved_ref):
    j = pl.program_id(0)
    col_block = emb_ref.shape[0]
    vocab_ids = lax.broadcasted_iota(jnp.int32, (col_block, row_block), 0)
    stats = (peak_ref, total_ref, moment_ref, chosen_ref)

    @pl.when(j == 0)
    def _():
        peak_ref[...] = jnp.full(peak_ref.shape, -1e30, jnp.float32)
        total_ref[...] = jnp.zeros(total_ref.shape, jnp.float32)
        moment_ref[...] = jnp.zeros(moment_ref.shape, jnp.float32)
        chosen_ref[...] = jnp.zeros(chosen_ref.shape, jnp.float32)

    def logits_of(rows):
        return lax.dot_general(
            emb_ref[...], normed_ref[rows, :], (((1,), (1,)), ((), ())),
            preferred_element_type=jnp.float32,
        )

    def add_chosen(rows, logits):
        local_id = ids_ref[:, rows] - j * col_block
        chosen_ref[:, rows] = chosen_ref[:, rows] + jnp.sum(
            jnp.where(vocab_ids == local_id, logits, 0.0), axis=0, keepdims=True
        )

    def rows_of(r):
        return pl.ds(pl.multiple_of(r * row_block, row_block), row_block)

    def exact_chunk(r, carry):
        rows = rows_of(r)
        logits = logits_of(rows)
        old_peak = peak_ref[:, rows]
        new_peak = jnp.maximum(old_peak, jnp.max(logits, axis=0, keepdims=True))
        weights = jnp.exp(logits - new_peak)
        scale = jnp.exp(old_peak - new_peak)
        total_ref[:, rows] = total_ref[:, rows] * scale + jnp.sum(weights, axis=0, keepdims=True)
        moment_ref[:, rows] = moment_ref[:, rows] * scale + jnp.sum(weights * logits, axis=0, keepdims=True)
        peak_ref[:, rows] = new_peak
        add_chosen(rows, logits)
        return carry

    def fast_chunk(r, worst):
        rows = rows_of(r)
        logits = logits_of(rows)
        old_peak = peak_ref[:, rows]
        shift = old_peak + LIFT
        tile_peak = jnp.max(logits, axis=0, keepdims=True)
        weights = jnp.exp(logits - shift)
        new_peak = jnp.maximum(old_peak, tile_peak)
        scale = jnp.exp(old_peak - new_peak)
        part_scale = jnp.exp(shift - new_peak)
        total_ref[:, rows] = total_ref[:, rows] * scale + jnp.sum(weights, axis=0, keepdims=True) * part_scale
        moment_ref[:, rows] = moment_ref[:, rows] * scale + jnp.sum(weights * logits, axis=0, keepdims=True) * part_scale
        peak_ref[:, rows] = new_peak
        add_chosen(rows, logits)
        return jnp.maximum(worst, tile_peak - old_peak)

    n_chunks = normed_ref.shape[0] // row_block

    @pl.when(j == 0)
    def _():
        lax.fori_loop(0, n_chunks, exact_chunk, 0, unroll=True)

    @pl.when(j > 0)
    def _():
        for k, ref in enumerate(stats):
            saved_ref[k:k + 1, :] = ref[...]
        worst = lax.fori_loop(
            0, n_chunks, fast_chunk, jnp.full((1, row_block), -1e30, jnp.float32), unroll=True
        )

        @pl.when(jnp.max(worst) > SAFE)
        def _():
            for k, ref in enumerate(stats):
                ref[...] = saved_ref[k:k + 1, :]
            lax.fori_loop(0, n_chunks, exact_chunk, 0, unroll=True)


def shard_stats(normed, embedding, in_shard_id, col_block=1024, row_block=256):
    rows, width = normed.shape
    vocab = embedding.shape[0]
    col_block = min(col_block, vocab)
    row_block = min(row_block, rows)
    stat = jax.ShapeDtypeStruct((1, rows), jnp.float32)
    resident = pl.BlockSpec((1, rows), lambda j: (0, 0))
    outs = pl.pallas_call(
        functools.partial(stats_kernel, row_block),
        grid=(vocab // col_block,),
        in_specs=[
            pl.BlockSpec((rows, width), lambda j: (0, 0)),
            pl.BlockSpec((col_block, width), lambda j: (j, 0)),
            pl.BlockSpec((1, rows), lambda j: (0, 0)),
        ],
        out_specs=[resident] * 4,
        out_shape=[stat] * 4,
        scratch_shapes=[pltpu.VMEM((4, rows), jnp.float32)],
        compiler_params=pltpu.CompilerParams(
            dimension_semantics=("arbitrary",), vmem_limit_bytes=48 * 1024 * 1024
        ),
        cost_estimate=pl.CostEstimate(
            flops=2 * rows * vocab * width,
            transcendentals=rows * vocab,
            bytes_accessed=rows * width * 2 + vocab * width * 2 + rows * 20,
        ),
    )(normed, embedding, in_shard_id[None, :])
    return jnp.concatenate(outs, axis=0)


def body(final_states, norm_gain, embedding, targets, deal):
    owners = lax.axis_size("req")
    own_rows = final_states.shape[0]
    shard_cols = embedding.shape[0]
    vocab_start = lax.axis_index("tp") * shard_cols
    member = (deal[:, None] // own_rows == jnp.arange(owners, dtype=jnp.int32)[None, :])
    counts = lax.all_gather(jnp.sum(member.astype(jnp.int32), axis=0), "req")
    live_count = jnp.sum(counts[:, lax.axis_index("req")])
    live = jnp.arange(own_rows, dtype=jnp.int32) < live_count

    normed = rms_normed(final_states, norm_gain)
    stats = shard_stats(normed, embedding, targets - vocab_start)
    group = lax.axis_size("tp")
    pieces = [stats]
    for shift in range(1, group):
        pieces.append(
            lax.ppermute(stats, "tp", [(d, (d + shift) % group) for d in range(group)])
        )
    gathered = jnp.stack(pieces)
    peaks = gathered[:, 0]
    row_peak = jnp.max(peaks, axis=0)
    scale = jnp.exp(peaks - row_peak[None, :])
    exp_total = jnp.sum(gathered[:, 1] * scale, axis=0)
    moment = jnp.sum(gathered[:, 2] * scale, axis=0)
    chosen = jnp.sum(gathered[:, 3], axis=0)
    log_total = row_peak + jnp.log(exp_total)
    expected = moment / exp_total
    logprob = jnp.where(live, chosen - log_total, 0.0)
    entropy = jnp.where(live, log_total - expected, 0.0)
    return (logprob, entropy)


def solution(mesh):
    return jax.shard_map(
        body,
        mesh=mesh,
        in_specs=(P("req", None), P(), P("tp", None), P("req"), P("req")),
        out_specs=(P("req"), P("req")),
        check_vma=False,
    )
```

```python
import functools

import jax
import jax.numpy as jnp
from jax import lax
from jax.experimental import pallas as pl
from jax.experimental.pallas import tpu as pltpu
from jax.sharding import PartitionSpec as P


def rms_normed(states, norm_gain):
    mean_square = jnp.mean(states * states, axis=1, keepdims=True)
    return (states * lax.rsqrt(mean_square + 1e-06) * norm_gain[None, :]).astype(jnp.bfloat16)


def shard_stats_xla(normed, embedding, in_shard_id):
    logits = lax.dot_general(
        normed, embedding, (((1,), (1,)), ((), ())), preferred_element_type=jnp.float32
    )
    peak = jnp.max(logits, axis=1)
    weights = jnp.exp(logits - peak[:, None])
    total = jnp.sum(weights, axis=1)
    moment = jnp.sum(weights * logits, axis=1)
    cols = lax.broadcasted_iota(jnp.int32, logits.shape, 1)
    chosen = jnp.sum(jnp.where(cols == in_shard_id[:, None], logits, 0.0), axis=1)
    return jnp.stack((peak, total, moment, chosen))


LIFT = 40.0
SAFE = 60.0


def stats_kernel(row_block, states_ref, gain_ref, emb_ref, ids_ref, peak_ref, total_ref, moment_ref, chosen_ref, normed_ref, saved_ref):
    j = pl.program_id(0)
    col_block = emb_ref.shape[0]
    vocab_ids = lax.broadcasted_iota(jnp.int32, (col_block, row_block), 0)
    stats = (peak_ref, total_ref, moment_ref, chosen_ref)

    @pl.when(j == 0)
    def _():
        for r in range(normed_ref.shape[0] // row_block):
            rows = pl.ds(r * row_block, row_block)
            x = states_ref[rows, :]
            mean_square = jnp.mean(x * x, axis=1, keepdims=True)
            normed_ref[rows, :] = (x * lax.rsqrt(mean_square + 1e-06) * gain_ref[...]).astype(jnp.bfloat16)
        peak_ref[...] = jnp.full(peak_ref.shape, -1e30, jnp.float32)
        total_ref[...] = jnp.zeros(total_ref.shape, jnp.float32)
        moment_ref[...] = jnp.zeros(moment_ref.shape, jnp.float32)
        chosen_ref[...] = jnp.zeros(chosen_ref.shape, jnp.float32)

    def logits_of(rows):
        return lax.dot_general(
            emb_ref[...], normed_ref[rows, :], (((1,), (1,)), ((), ())),
            preferred_element_type=jnp.float32,
        )

    def add_chosen(rows, logits):
        local_id = ids_ref[:, rows] - j * col_block
        chosen_ref[:, rows] = chosen_ref[:, rows] + jnp.sum(
            jnp.where(vocab_ids == local_id, logits, 0.0), axis=0, keepdims=True
        )

    def rows_of(r):
        return pl.ds(pl.multiple_of(r * row_block, row_block), row_block)

    def exact_chunk(r, carry):
        rows = rows_of(r)
        logits = logits_of(rows)
        old_peak = peak_ref[:, rows]
        new_peak = jnp.maximum(old_peak, jnp.max(logits, axis=0, keepdims=True))
        weights = jnp.exp(logits - new_peak)
        scale = jnp.exp(old_peak - new_peak)
        total_ref[:, rows] = total_ref[:, rows] * scale + jnp.sum(weights, axis=0, keepdims=True)
        moment_ref[:, rows] = moment_ref[:, rows] * scale + jnp.sum(weights * logits, axis=0, keepdims=True)
        peak_ref[:, rows] = new_peak
        add_chosen(rows, logits)
        return carry

    def fast_chunk(r, worst):
        rows = rows_of(r)
        logits = logits_of(rows)
        old_peak = peak_ref[:, rows]
        shift = old_peak + LIFT
        tile_peak = jnp.max(logits, axis=0, keepdims=True)
        weights = jnp.exp(logits - shift)
        new_peak = jnp.maximum(old_peak, tile_peak)
        scale = jnp.exp(old_peak - new_peak)
        part_scale = jnp.exp(shift - new_peak)
        total_ref[:, rows] = total_ref[:, rows] * scale + jnp.sum(weights, axis=0, keepdims=True) * part_scale
        moment_ref[:, rows] = moment_ref[:, rows] * scale + jnp.sum(weights * logits, axis=0, keepdims=True) * part_scale
        peak_ref[:, rows] = new_peak
        add_chosen(rows, logits)
        return jnp.maximum(worst, tile_peak - old_peak)

    n_chunks = normed_ref.shape[0] // row_block

    @pl.when(j == 0)
    def _():
        lax.fori_loop(0, n_chunks, exact_chunk, 0, unroll=True)

    @pl.when(j > 0)
    def _():
        for k, ref in enumerate(stats):
            saved_ref[k:k + 1, :] = ref[...]
        worst = lax.fori_loop(
            0, n_chunks, fast_chunk, jnp.full((1, row_block), -1e30, jnp.float32), unroll=True
        )

        @pl.when(jnp.max(worst) > SAFE)
        def _():
            for k, ref in enumerate(stats):
                ref[...] = saved_ref[k:k + 1, :]
            lax.fori_loop(0, n_chunks, exact_chunk, 0, unroll=True)


def shard_stats(states, norm_gain, embedding, in_shard_id, col_block=1024, row_block=256):
    rows, width = states.shape
    vocab = embedding.shape[0]
    col_block = min(col_block, vocab)
    row_block = min(row_block, rows)
    stat = jax.ShapeDtypeStruct((1, rows), jnp.float32)
    resident = pl.BlockSpec((1, rows), lambda j: (0, 0))
    outs = pl.pallas_call(
        functools.partial(stats_kernel, row_block),
        grid=(vocab // col_block,),
        in_specs=[
            pl.BlockSpec((rows, width), lambda j: (0, 0)),
            pl.BlockSpec((1, width), lambda j: (0, 0)),
            pl.BlockSpec((col_block, width), lambda j: (j, 0)),
            pl.BlockSpec((1, rows), lambda j: (0, 0)),
        ],
        out_specs=[resident] * 4,
        out_shape=[stat] * 4,
        scratch_shapes=[pltpu.VMEM((rows, width), jnp.bfloat16), pltpu.VMEM((4, rows), jnp.float32)],
        compiler_params=pltpu.CompilerParams(
            dimension_semantics=("arbitrary",), vmem_limit_bytes=60 * 1024 * 1024
        ),
        cost_estimate=pl.CostEstimate(
            flops=2 * rows * vocab * width,
            transcendentals=rows * vocab,
            bytes_accessed=rows * width * 4 + vocab * width * 2 + rows * 20,
        ),
    )(states, norm_gain[None, :], embedding, in_shard_id[None, :])
    return jnp.concatenate(outs, axis=0)


def body(final_states, norm_gain, embedding, targets, deal):
    owners = lax.axis_size("req")
    own_rows = final_states.shape[0]
    shard_cols = embedding.shape[0]
    vocab_start = lax.axis_index("tp") * shard_cols
    member = (deal[:, None] // own_rows == jnp.arange(owners, dtype=jnp.int32)[None, :])
    counts = lax.all_gather(jnp.sum(member.astype(jnp.int32), axis=0), "req")
    live_count = jnp.sum(counts[:, lax.axis_index("req")])
    live = jnp.arange(own_rows, dtype=jnp.int32) < live_count

    stats = shard_stats(final_states, norm_gain, embedding, targets - vocab_start)
    group = lax.axis_size("tp")
    pieces = [stats]
    for shift in range(1, group):
        pieces.append(
            lax.ppermute(stats, "tp", [(d, (d + shift) % group) for d in range(group)])
        )
    gathered = jnp.stack(pieces)
    peaks = gathered[:, 0]
    row_peak = jnp.max(peaks, axis=0)
    scale = jnp.exp(peaks - row_peak[None, :])
    exp_total = jnp.sum(gathered[:, 1] * scale, axis=0)
    moment = jnp.sum(gathered[:, 2] * scale, axis=0)
    chosen = jnp.sum(gathered[:, 3], axis=0)
    log_total = row_peak + jnp.log(exp_total)
    expected = moment / exp_total
    logprob = jnp.where(live, chosen - log_total, 0.0)
    entropy = jnp.where(live, log_total - expected, 0.0)
    return (logprob, entropy)


def solution(mesh):
    return jax.shard_map(
        body,
        mesh=mesh,
        in_specs=(P("req", None), P(), P("tp", None), P("req"), P("req")),
        out_specs=(P("req"), P("req")),
        check_vma=False,
    )
```

```python
import functools

import jax
import jax.numpy as jnp
from jax import lax
from jax.experimental import pallas as pl
from jax.experimental.pallas import tpu as pltpu
from jax.sharding import PartitionSpec as P


def rms_normed(states, norm_gain):
    mean_square = jnp.mean(states * states, axis=1, keepdims=True)
    return (states * lax.rsqrt(mean_square + 1e-06) * norm_gain[None, :]).astype(jnp.bfloat16)


def shard_stats_xla(normed, embedding, in_shard_id):
    logits = lax.dot_general(
        normed, embedding, (((1,), (1,)), ((), ())), preferred_element_type=jnp.float32
    )
    peak = jnp.max(logits, axis=1)
    weights = jnp.exp(logits - peak[:, None])
    total = jnp.sum(weights, axis=1)
    moment = jnp.sum(weights * logits, axis=1)
    cols = lax.broadcasted_iota(jnp.int32, logits.shape, 1)
    chosen = jnp.sum(jnp.where(cols == in_shard_id[:, None], logits, 0.0), axis=1)
    return jnp.stack((peak, total, moment, chosen))


LIFT = 40.0
SAFE = 60.0


def stats_kernel(row_block, states_ref, gain_ref, emb_ref, ids_ref, stats_ref, normed_ref, saved_ref):
    j = pl.program_id(0)
    col_block = emb_ref.shape[0]
    vocab_ids = lax.broadcasted_iota(jnp.int32, (col_block, row_block), 0)
    peak_ref, total_ref, moment_ref, chosen_ref = (stats_ref.at[k:k + 1] for k in range(4))

    @pl.when(j == 0)
    def _():
        for r in range(normed_ref.shape[0] // row_block):
            rows = pl.ds(r * row_block, row_block)
            x = states_ref[rows, :]
            mean_square = jnp.mean(x * x, axis=1, keepdims=True)
            normed_ref[rows, :] = (x * lax.rsqrt(mean_square + 1e-06) * gain_ref[...]).astype(jnp.bfloat16)
        peak_ref[...] = jnp.full(peak_ref.shape, -1e30, jnp.float32)
        total_ref[...] = jnp.zeros(total_ref.shape, jnp.float32)
        moment_ref[...] = jnp.zeros(moment_ref.shape, jnp.float32)
        chosen_ref[...] = jnp.zeros(chosen_ref.shape, jnp.float32)

    def logits_of(rows):
        return lax.dot_general(
            emb_ref[...], normed_ref[rows, :], (((1,), (1,)), ((), ())),
            preferred_element_type=jnp.float32,
        )

    def add_chosen(rows, logits):
        local_id = ids_ref[:, rows] - j * col_block
        chosen_ref[:, rows] = chosen_ref[:, rows] + jnp.sum(
            jnp.where(vocab_ids == local_id, logits, 0.0), axis=0, keepdims=True
        )

    def rows_of(r):
        return pl.ds(pl.multiple_of(r * row_block, row_block), row_block)

    def exact_chunk(r, carry):
        rows = rows_of(r)
        logits = logits_of(rows)
        old_peak = peak_ref[:, rows]
        new_peak = jnp.maximum(old_peak, jnp.max(logits, axis=0, keepdims=True))
        weights = jnp.exp(logits - new_peak)
        scale = jnp.exp(old_peak - new_peak)
        total_ref[:, rows] = total_ref[:, rows] * scale + jnp.sum(weights, axis=0, keepdims=True)
        moment_ref[:, rows] = moment_ref[:, rows] * scale + jnp.sum(weights * logits, axis=0, keepdims=True)
        peak_ref[:, rows] = new_peak
        add_chosen(rows, logits)
        return carry

    def fast_chunk(r, worst):
        rows = rows_of(r)
        logits = logits_of(rows)
        old_peak = peak_ref[:, rows]
        shift = old_peak + LIFT
        tile_peak = jnp.max(logits, axis=0, keepdims=True)
        weights = jnp.exp(logits - shift)
        new_peak = jnp.maximum(old_peak, tile_peak)
        scale = jnp.exp(old_peak - new_peak)
        part_scale = jnp.exp(shift - new_peak)
        total_ref[:, rows] = total_ref[:, rows] * scale + jnp.sum(weights, axis=0, keepdims=True) * part_scale
        moment_ref[:, rows] = moment_ref[:, rows] * scale + jnp.sum(weights * logits, axis=0, keepdims=True) * part_scale
        peak_ref[:, rows] = new_peak
        add_chosen(rows, logits)
        return jnp.maximum(worst, tile_peak - old_peak)

    n_chunks = normed_ref.shape[0] // row_block

    @pl.when(j == 0)
    def _():
        lax.fori_loop(0, n_chunks, exact_chunk, 0, unroll=True)

    @pl.when(j > 0)
    def _():
        saved_ref[...] = stats_ref[...]
        worst = lax.fori_loop(
            0, n_chunks, fast_chunk, jnp.full((1, row_block), -1e30, jnp.float32), unroll=True
        )

        @pl.when(jnp.max(worst) > SAFE)
        def _():
            stats_ref[...] = saved_ref[...]
            lax.fori_loop(0, n_chunks, exact_chunk, 0, unroll=True)


def shard_stats(states, norm_gain, embedding, in_shard_id, col_block=1024, row_block=256):
    rows, width = states.shape
    vocab = embedding.shape[0]
    col_block = min(col_block, vocab)
    row_block = min(row_block, rows)
    stat = jax.ShapeDtypeStruct((4, rows), jnp.float32)
    resident = pl.BlockSpec((4, rows), lambda j: (0, 0))
    outs = pl.pallas_call(
        functools.partial(stats_kernel, row_block),
        grid=(vocab // col_block,),
        in_specs=[
            pl.BlockSpec((rows, width), lambda j: (0, 0)),
            pl.BlockSpec((1, width), lambda j: (0, 0)),
            pl.BlockSpec((col_block, width), lambda j: (j, 0)),
            pl.BlockSpec((1, rows), lambda j: (0, 0)),
        ],
        out_specs=resident,
        out_shape=stat,
        scratch_shapes=[pltpu.VMEM((rows, width), jnp.bfloat16), pltpu.VMEM((4, rows), jnp.float32)],
        compiler_params=pltpu.CompilerParams(
            dimension_semantics=("arbitrary",), vmem_limit_bytes=60 * 1024 * 1024
        ),
        cost_estimate=pl.CostEstimate(
            flops=2 * rows * vocab * width,
            transcendentals=rows * vocab,
            bytes_accessed=rows * width * 4 + vocab * width * 2 + rows * 20,
        ),
    )(states, norm_gain[None, :], embedding, in_shard_id[None, :])
    return outs


def body(final_states, norm_gain, embedding, targets, deal):
    owners = lax.axis_size("req")
    own_rows = final_states.shape[0]
    shard_cols = embedding.shape[0]
    vocab_start = lax.axis_index("tp") * shard_cols
    member = (jnp.arange(owners, dtype=jnp.int32)[:, None] == (deal // own_rows)[None, :])
    counts = lax.all_gather(jnp.sum(member.astype(jnp.int32), axis=1), "req")
    live_count = jnp.sum(counts[:, lax.axis_index("req")])
    live = jnp.arange(own_rows, dtype=jnp.int32) < live_count

    stats = shard_stats(final_states, norm_gain, embedding, targets - vocab_start)
    group = lax.axis_size("tp")
    pieces = [stats]
    for shift in range(1, group):
        pieces.append(
            lax.ppermute(stats, "tp", [(d, (d + shift) % group) for d in range(group)])
        )
    gathered = jnp.stack(pieces)
    peaks = gathered[:, 0]
    row_peak = jnp.max(peaks, axis=0)
    scale = jnp.exp(peaks - row_peak[None, :])
    exp_total = jnp.sum(gathered[:, 1] * scale, axis=0)
    moment = jnp.sum(gathered[:, 2] * scale, axis=0)
    chosen = jnp.sum(gathered[:, 3], axis=0)
    log_total = row_peak + jnp.log(exp_total)
    expected = moment / exp_total
    logprob = jnp.where(live, chosen - log_total, 0.0)
    entropy = jnp.where(live, log_total - expected, 0.0)
    return (logprob, entropy)


def solution(mesh):
    return jax.shard_map(
        body,
        mesh=mesh,
        in_specs=(P("req", None), P(), P("tp", None), P("req"), P("req")),
        out_specs=(P("req"), P("req")),
        check_vma=False,
    )
```

```python
import functools

import jax
import jax.numpy as jnp
from jax import lax
from jax.experimental import pallas as pl
from jax.experimental.pallas import tpu as pltpu
from jax.sharding import PartitionSpec as P


def rms_normed(states, norm_gain):
    mean_square = jnp.mean(states * states, axis=1, keepdims=True)
    return (states * lax.rsqrt(mean_square + 1e-06) * norm_gain[None, :]).astype(jnp.bfloat16)


def shard_stats_xla(normed, embedding, in_shard_id):
    logits = lax.dot_general(
        normed, embedding, (((1,), (1,)), ((), ())), preferred_element_type=jnp.float32
    )
    peak = jnp.max(logits, axis=1)
    weights = jnp.exp(logits - peak[:, None])
    total = jnp.sum(weights, axis=1)
    moment = jnp.sum(weights * logits, axis=1)
    cols = lax.broadcasted_iota(jnp.int32, logits.shape, 1)
    chosen = jnp.sum(jnp.where(cols == in_shard_id[:, None], logits, 0.0), axis=1)
    return jnp.stack((peak, total, moment, chosen))


LIFT = 40.0
SAFE = 60.0


def stats_kernel(row_block, states_ref, gain_ref, emb_ref, ids_ref, stats_ref, normed_ref, saved_ref):
    j = pl.program_id(0)
    col_block = emb_ref.shape[0]
    vocab_ids = lax.broadcasted_iota(jnp.int32, (col_block, row_block), 0)
    peak_ref, total_ref, moment_ref, chosen_ref = (stats_ref.at[k:k + 1] for k in range(4))

    @pl.when(j == 0)
    def _():
        for r in range(normed_ref.shape[0] // row_block):
            rows = pl.ds(r * row_block, row_block)
            x = states_ref[rows, :]
            mean_square = jnp.mean(x * x, axis=1, keepdims=True)
            normed_ref[rows, :] = (x * lax.rsqrt(mean_square + 1e-06) * gain_ref[...]).astype(jnp.bfloat16)
        peak_ref[...] = jnp.full(peak_ref.shape, -1e30, jnp.float32)
        total_ref[...] = jnp.zeros(total_ref.shape, jnp.float32)
        moment_ref[...] = jnp.zeros(moment_ref.shape, jnp.float32)
        chosen_ref[...] = jnp.zeros(chosen_ref.shape, jnp.float32)

    def logits_of(rows):
        return lax.dot_general(
            emb_ref[...], normed_ref[rows, :], (((1,), (1,)), ((), ())),
            preferred_element_type=jnp.float32,
        )

    def add_chosen(rows, logits):
        local_id = ids_ref[:, rows] - (lax.axis_index("tp") * pl.num_programs(0) + j) * col_block
        chosen_ref[:, rows] = chosen_ref[:, rows] + jnp.sum(
            jnp.where(vocab_ids == local_id, logits, 0.0), axis=0, keepdims=True
        )

    def rows_of(r):
        return pl.ds(pl.multiple_of(r * row_block, row_block), row_block)

    def exact_chunk(r, carry):
        rows = rows_of(r)
        logits = logits_of(rows)
        old_peak = peak_ref[:, rows]
        new_peak = jnp.maximum(old_peak, jnp.max(logits, axis=0, keepdims=True))
        weights = jnp.exp(logits - new_peak)
        scale = jnp.exp(old_peak - new_peak)
        total_ref[:, rows] = total_ref[:, rows] * scale + jnp.sum(weights, axis=0, keepdims=True)
        moment_ref[:, rows] = moment_ref[:, rows] * scale + jnp.sum(weights * logits, axis=0, keepdims=True)
        peak_ref[:, rows] = new_peak
        add_chosen(rows, logits)
        return carry

    def fast_chunk(r, worst):
        rows = rows_of(r)
        logits = logits_of(rows)
        old_peak = peak_ref[:, rows]
        shift = old_peak + LIFT
        tile_peak = jnp.max(logits, axis=0, keepdims=True)
        weights = jnp.exp(logits - shift)
        new_peak = jnp.maximum(old_peak, tile_peak)
        scale = jnp.exp(old_peak - new_peak)
        part_scale = jnp.exp(shift - new_peak)
        total_ref[:, rows] = total_ref[:, rows] * scale + jnp.sum(weights, axis=0, keepdims=True) * part_scale
        moment_ref[:, rows] = moment_ref[:, rows] * scale + jnp.sum(weights * logits, axis=0, keepdims=True) * part_scale
        peak_ref[:, rows] = new_peak
        add_chosen(rows, logits)
        return jnp.maximum(worst, tile_peak - old_peak)

    n_chunks = normed_ref.shape[0] // row_block

    @pl.when(j == 0)
    def _():
        lax.fori_loop(0, n_chunks, exact_chunk, 0, unroll=True)

    @pl.when(j > 0)
    def _():
        saved_ref[...] = stats_ref[...]
        worst = lax.fori_loop(
            0, n_chunks, fast_chunk, jnp.full((1, row_block), -1e30, jnp.float32), unroll=True
        )

        @pl.when(jnp.max(worst) > SAFE)
        def _():
            stats_ref[...] = saved_ref[...]
            lax.fori_loop(0, n_chunks, exact_chunk, 0, unroll=True)


def shard_stats(states, norm_gain, embedding, in_shard_id, col_block=1024, row_block=256):
    rows, width = states.shape
    vocab = embedding.shape[0]
    col_block = min(col_block, vocab)
    row_block = min(row_block, rows)
    stat = jax.ShapeDtypeStruct((4, rows), jnp.float32)
    resident = pl.BlockSpec((4, rows), lambda j: (0, 0))
    outs = pl.pallas_call(
        functools.partial(stats_kernel, row_block),
        grid=(vocab // col_block,),
        in_specs=[
            pl.BlockSpec((rows, width), lambda j: (0, 0)),
            pl.BlockSpec((1, width), lambda j: (0, 0)),
            pl.BlockSpec((col_block, width), lambda j: (j, 0)),
            pl.BlockSpec((1, rows), lambda j: (0, 0)),
        ],
        out_specs=resident,
        out_shape=stat,
        scratch_shapes=[pltpu.VMEM((rows, width), jnp.bfloat16), pltpu.VMEM((4, rows), jnp.float32)],
        compiler_params=pltpu.CompilerParams(
            dimension_semantics=("arbitrary",), vmem_limit_bytes=60 * 1024 * 1024
        ),
        cost_estimate=pl.CostEstimate(
            flops=2 * rows * vocab * width,
            transcendentals=rows * vocab,
            bytes_accessed=rows * width * 4 + vocab * width * 2 + rows * 20,
        ),
    )(states, norm_gain[None, :], embedding, in_shard_id[None, :])
    return outs


def body(final_states, norm_gain, embedding, targets, deal):
    owners = lax.axis_size("req")
    own_rows = final_states.shape[0]
    shard_cols = embedding.shape[0]
    member = (jnp.arange(owners, dtype=jnp.int32)[:, None] == (deal // own_rows)[None, :])
    counts = lax.all_gather(jnp.sum(member.astype(jnp.int32), axis=1), "req")
    live_count = jnp.sum(counts[:, lax.axis_index("req")])
    live = jnp.arange(own_rows, dtype=jnp.int32) < live_count

    stats = shard_stats(final_states, norm_gain, embedding, targets)
    group = lax.axis_size("tp")
    pieces = [stats]
    for shift in range(1, group):
        pieces.append(
            lax.ppermute(stats, "tp", [(d, (d + shift) % group) for d in range(group)])
        )
    gathered = jnp.stack(pieces)
    peaks = gathered[:, 0]
    row_peak = jnp.max(peaks, axis=0)
    scale = jnp.exp(peaks - row_peak[None, :])
    exp_total = jnp.sum(gathered[:, 1] * scale, axis=0)
    moment = jnp.sum(gathered[:, 2] * scale, axis=0)
    chosen = jnp.sum(gathered[:, 3], axis=0)
    log_total = row_peak + jnp.log(exp_total)
    expected = moment / exp_total
    logprob = jnp.where(live, chosen - log_total, 0.0)
    entropy = jnp.where(live, log_total - expected, 0.0)
    return (logprob, entropy)


def solution(mesh):
    return jax.shard_map(
        body,
        mesh=mesh,
        in_specs=(P("req", None), P(), P("tp", None), P("req"), P("req")),
        out_specs=(P("req"), P("req")),
        check_vma=False,
    )
```

```python
import functools

import jax
import jax.numpy as jnp
from jax import lax
from jax.experimental import pallas as pl
from jax.experimental.pallas import tpu as pltpu
from jax.sharding import PartitionSpec as P


def rms_normed(states, norm_gain):
    mean_square = jnp.mean(states * states, axis=1, keepdims=True)
    return (states * lax.rsqrt(mean_square + 1e-06) * norm_gain[None, :]).astype(jnp.bfloat16)


def shard_stats_xla(normed, embedding, in_shard_id):
    logits = lax.dot_general(
        normed, embedding, (((1,), (1,)), ((), ())), preferred_element_type=jnp.float32
    )
    peak = jnp.max(logits, axis=1)
    weights = jnp.exp(logits - peak[:, None])
    total = jnp.sum(weights, axis=1)
    moment = jnp.sum(weights * logits, axis=1)
    cols = lax.broadcasted_iota(jnp.int32, logits.shape, 1)
    chosen = jnp.sum(jnp.where(cols == in_shard_id[:, None], logits, 0.0), axis=1)
    return jnp.stack((peak, total, moment, chosen))


LIFT = 40.0
SAFE = 60.0


def stats_kernel(row_block, states_ref, gain_ref, emb_ref, ids_ref, stats_ref, normed_ref, saved_ref):
    j = pl.program_id(0)
    col_block = emb_ref.shape[0]
    vocab_ids = lax.broadcasted_iota(jnp.int32, (col_block, row_block), 0)
    peak_ref, total_ref, moment_ref, chosen_ref = (stats_ref.at[k:k + 1] for k in range(4))

    @pl.when(j == 0)
    def _():
        for r in range(normed_ref.shape[0] // row_block):
            rows = pl.ds(r * row_block, row_block)
            x = states_ref[rows, :]
            mean_square = jnp.mean(x * x, axis=1, keepdims=True)
            normed_ref[rows, :] = (x * lax.rsqrt(mean_square + 1e-06) * gain_ref[...]).astype(jnp.bfloat16)
        peak_ref[...] = jnp.full(peak_ref.shape, -1e30, jnp.float32)
        total_ref[...] = jnp.zeros(total_ref.shape, jnp.float32)
        moment_ref[...] = jnp.zeros(moment_ref.shape, jnp.float32)
        chosen_ref[...] = jnp.zeros(chosen_ref.shape, jnp.float32)

    def logits_of(rows):
        return lax.dot_general(
            emb_ref[...], normed_ref[rows, :], (((1,), (1,)), ((), ())),
            preferred_element_type=jnp.float32,
        )

    def add_chosen(rows, logits):
        local_id = ids_ref[:, rows] - (lax.axis_index("tp") * pl.num_programs(0) + j) * col_block
        chosen_ref[:, rows] = chosen_ref[:, rows] + jnp.sum(
            jnp.where(vocab_ids == local_id, logits, 0.0), axis=0, keepdims=True
        )

    def rows_of(r):
        return pl.ds(pl.multiple_of(r * row_block, row_block), row_block)

    def exact_chunk(r, carry):
        rows = rows_of(r)
        logits = logits_of(rows)
        old_peak = peak_ref[:, rows]
        new_peak = jnp.maximum(old_peak, jnp.max(logits, axis=0, keepdims=True))
        weights = jnp.exp(logits - new_peak)
        scale = jnp.exp(old_peak - new_peak)
        total_ref[:, rows] = total_ref[:, rows] * scale + jnp.sum(weights, axis=0, keepdims=True)
        moment_ref[:, rows] = moment_ref[:, rows] * scale + jnp.sum(weights * logits, axis=0, keepdims=True)
        peak_ref[:, rows] = new_peak
        add_chosen(rows, logits)
        return carry

    def fast_chunk(r, worst):
        rows = rows_of(r)
        logits = logits_of(rows)
        old_peak = peak_ref[:, rows]
        shift = old_peak + LIFT
        tile_peak = jnp.max(logits, axis=0, keepdims=True)
        weights = jnp.exp(logits - shift)
        new_peak = jnp.maximum(old_peak, tile_peak)
        scale = jnp.exp(old_peak - new_peak)
        part_scale = jnp.exp(shift - new_peak)
        total_ref[:, rows] = total_ref[:, rows] * scale + jnp.sum(weights, axis=0, keepdims=True) * part_scale
        moment_ref[:, rows] = moment_ref[:, rows] * scale + jnp.sum(weights * logits, axis=0, keepdims=True) * part_scale
        peak_ref[:, rows] = new_peak
        add_chosen(rows, logits)
        return jnp.maximum(worst, tile_peak - old_peak)

    n_chunks = normed_ref.shape[0] // row_block

    @pl.when(j == 0)
    def _():
        lax.fori_loop(0, n_chunks, exact_chunk, 0, unroll=True)

    @pl.when(j > 0)
    def _():
        saved_ref[...] = stats_ref[...]
        worst = lax.fori_loop(
            0, n_chunks, fast_chunk, jnp.full((1, row_block), -1e30, jnp.float32), unroll=True
        )

        @pl.when(jnp.max(worst) > SAFE)
        def _():
            stats_ref[...] = saved_ref[...]
            lax.fori_loop(0, n_chunks, exact_chunk, 0, unroll=True)


def shard_stats(states, norm_gain, embedding, in_shard_id, col_block=1024, row_block=256):
    rows, width = states.shape
    vocab = embedding.shape[0]
    col_block = min(col_block, vocab)
    row_block = min(row_block, rows)
    stat = jax.ShapeDtypeStruct((4, rows), jnp.float32)
    resident = pl.BlockSpec((4, rows), lambda j: (0, 0))
    outs = pl.pallas_call(
        functools.partial(stats_kernel, row_block),
        grid=(vocab // col_block,),
        in_specs=[
            pl.BlockSpec((rows, width), lambda j: (0, 0)),
            pl.BlockSpec((1, width), lambda j: (0, 0)),
            pl.BlockSpec((col_block, width), lambda j: (j, 0)),
            pl.BlockSpec((1, rows), lambda j: (0, 0)),
        ],
        out_specs=resident,
        out_shape=stat,
        scratch_shapes=[pltpu.VMEM((rows, width), jnp.bfloat16), pltpu.VMEM((4, rows), jnp.float32)],
        compiler_params=pltpu.CompilerParams(
            dimension_semantics=("arbitrary",), vmem_limit_bytes=60 * 1024 * 1024
        ),
        cost_estimate=pl.CostEstimate(
            flops=2 * rows * vocab * width,
            transcendentals=rows * vocab,
            bytes_accessed=rows * width * 4 + vocab * width * 2 + rows * 20,
        ),
    )(states, norm_gain[None, :], embedding, in_shard_id[None, :])
    return outs


def body(final_states, norm_gain, embedding, targets, deal):
    owners = lax.axis_size("req")
    own_rows = final_states.shape[0]
    shard_cols = embedding.shape[0]
    member = (jnp.arange(owners, dtype=jnp.int32)[:, None] == (deal // own_rows)[None, :])
    local_counts = jnp.sum(member.astype(jnp.int32), axis=1)
    first_copy = lax.axis_index("tp") == 0
    counts = lax.psum(jnp.where(first_copy, local_counts, 0), ("req", "tp"))
    live_count = counts[lax.axis_index("req")]
    live = jnp.arange(own_rows, dtype=jnp.int32) < live_count

    stats = shard_stats(final_states, norm_gain, embedding, targets)
    group = lax.axis_size("tp")
    pieces = [stats]
    for shift in range(1, group):
        pieces.append(
            lax.ppermute(stats, "tp", [(d, (d + shift) % group) for d in range(group)])
        )
    gathered = jnp.stack(pieces)
    peaks = gathered[:, 0]
    row_peak = jnp.max(peaks, axis=0)
    scale = jnp.exp(peaks - row_peak[None, :])
    exp_total = jnp.sum(gathered[:, 1] * scale, axis=0)
    moment = jnp.sum(gathered[:, 2] * scale, axis=0)
    chosen = jnp.sum(gathered[:, 3], axis=0)
    log_total = row_peak + jnp.log(exp_total)
    expected = moment / exp_total
    logprob = jnp.where(live, chosen - log_total, 0.0)
    entropy = jnp.where(live, log_total - expected, 0.0)
    return (logprob, entropy)


def solution(mesh):
    return jax.shard_map(
        body,
        mesh=mesh,
        in_specs=(P("req", None), P(), P("tp", None), P("req"), P("req")),
        out_specs=(P("req"), P("req")),
        check_vma=False,
    )
```

```python
import functools

import jax
import jax.numpy as jnp
from jax import lax
from jax.experimental import pallas as pl
from jax.experimental.pallas import tpu as pltpu
from jax.sharding import PartitionSpec as P


def rms_normed(states, norm_gain):
    mean_square = jnp.mean(states * states, axis=1, keepdims=True)
    return (states * lax.rsqrt(mean_square + 1e-06) * norm_gain[None, :]).astype(jnp.bfloat16)


def shard_stats_xla(normed, embedding, in_shard_id):
    logits = lax.dot_general(
        normed, embedding, (((1,), (1,)), ((), ())), preferred_element_type=jnp.float32
    )
    peak = jnp.max(logits, axis=1)
    weights = jnp.exp(logits - peak[:, None])
    total = jnp.sum(weights, axis=1)
    moment = jnp.sum(weights * logits, axis=1)
    cols = lax.broadcasted_iota(jnp.int32, logits.shape, 1)
    chosen = jnp.sum(jnp.where(cols == in_shard_id[:, None], logits, 0.0), axis=1)
    return jnp.stack((peak, total, moment, chosen))


LIFT = 40.0
SAFE = 60.0


def stats_kernel(row_block, states_ref, gain_ref, emb_ref, ids_ref, stats_ref, normed_ref, saved_ref, states_vmem, copy_sems):
    j = pl.program_id(0)
    col_block = emb_ref.shape[0]
    vocab_ids = lax.broadcasted_iota(jnp.int32, (col_block, row_block), 0)
    peak_ref, total_ref, moment_ref, chosen_ref = (stats_ref.at[k:k + 1] for k in range(4))

    @pl.when(j == 0)
    def _():
        copies = [
            pltpu.make_async_copy(
                states_ref.at[pl.ds(r * row_block, row_block)],
                states_vmem.at[pl.ds(r * row_block, row_block)],
                copy_sems.at[r],
            )
            for r in range(normed_ref.shape[0] // row_block)
        ]
        for copy in copies:
            copy.start()
        for r, copy in enumerate(copies):
            rows = pl.ds(r * row_block, row_block)
            copy.wait()
            x = states_vmem[rows, :]
            mean_square = jnp.mean(x * x, axis=1, keepdims=True)
            normed_ref[rows, :] = (x * lax.rsqrt(mean_square + 1e-06) * gain_ref[...]).astype(jnp.bfloat16)
        peak_ref[...] = jnp.full(peak_ref.shape, -1e30, jnp.float32)
        total_ref[...] = jnp.zeros(total_ref.shape, jnp.float32)
        moment_ref[...] = jnp.zeros(moment_ref.shape, jnp.float32)
        chosen_ref[...] = jnp.zeros(chosen_ref.shape, jnp.float32)

    def logits_of(rows):
        return lax.dot_general(
            emb_ref[...], normed_ref[rows, :], (((1,), (1,)), ((), ())),
            preferred_element_type=jnp.float32,
        )

    def add_chosen(rows, logits):
        local_id = ids_ref[:, rows] - (lax.axis_index("tp") * pl.num_programs(0) + j) * col_block
        chosen_ref[:, rows] = chosen_ref[:, rows] + jnp.sum(
            jnp.where(vocab_ids == local_id, logits, 0.0), axis=0, keepdims=True
        )

    def rows_of(r):
        return pl.ds(pl.multiple_of(r * row_block, row_block), row_block)

    def exact_chunk(r, carry):
        rows = rows_of(r)
        logits = logits_of(rows)
        old_peak = peak_ref[:, rows]
        new_peak = jnp.maximum(old_peak, jnp.max(logits, axis=0, keepdims=True))
        weights = jnp.exp(logits - new_peak)
        scale = jnp.exp(old_peak - new_peak)
        total_ref[:, rows] = total_ref[:, rows] * scale + jnp.sum(weights, axis=0, keepdims=True)
        moment_ref[:, rows] = moment_ref[:, rows] * scale + jnp.sum(weights * logits, axis=0, keepdims=True)
        peak_ref[:, rows] = new_peak
        add_chosen(rows, logits)
        return carry

    def fast_chunk(r, worst):
        rows = rows_of(r)
        logits = logits_of(rows)
        old_peak = peak_ref[:, rows]
        shift = old_peak + LIFT
        tile_peak = jnp.max(logits, axis=0, keepdims=True)
        weights = jnp.exp(logits - shift)
        new_peak = jnp.maximum(old_peak, tile_peak)
        scale = jnp.exp(old_peak - new_peak)
        part_scale = jnp.exp(shift - new_peak)
        total_ref[:, rows] = total_ref[:, rows] * scale + jnp.sum(weights, axis=0, keepdims=True) * part_scale
        moment_ref[:, rows] = moment_ref[:, rows] * scale + jnp.sum(weights * logits, axis=0, keepdims=True) * part_scale
        peak_ref[:, rows] = new_peak
        add_chosen(rows, logits)
        return jnp.maximum(worst, tile_peak - old_peak)

    n_chunks = normed_ref.shape[0] // row_block

    @pl.when(j == 0)
    def _():
        lax.fori_loop(0, n_chunks, exact_chunk, 0, unroll=True)

    @pl.when(j > 0)
    def _():
        saved_ref[...] = stats_ref[...]
        worst = lax.fori_loop(
            0, n_chunks, fast_chunk, jnp.full((1, row_block), -1e30, jnp.float32), unroll=True
        )

        @pl.when(jnp.max(worst) > SAFE)
        def _():
            stats_ref[...] = saved_ref[...]
            lax.fori_loop(0, n_chunks, exact_chunk, 0, unroll=True)


def shard_stats(states, norm_gain, embedding, in_shard_id, col_block=1024, row_block=256):
    rows, width = states.shape
    vocab = embedding.shape[0]
    col_block = min(col_block, vocab)
    row_block = min(row_block, rows)
    stat = jax.ShapeDtypeStruct((4, rows), jnp.float32)
    resident = pl.BlockSpec((4, rows), lambda j: (0, 0))
    outs = pl.pallas_call(
        functools.partial(stats_kernel, row_block),
        grid=(vocab // col_block,),
        in_specs=[
            pl.BlockSpec(memory_space=pl.ANY),
            pl.BlockSpec((1, width), lambda j: (0, 0)),
            pl.BlockSpec((col_block, width), lambda j: (j, 0)),
            pl.BlockSpec((1, rows), lambda j: (0, 0)),
        ],
        out_specs=resident,
        out_shape=stat,
        scratch_shapes=[
            pltpu.VMEM((rows, width), jnp.bfloat16),
            pltpu.VMEM((4, rows), jnp.float32),
            pltpu.VMEM((rows, width), jnp.float32),
            pltpu.SemaphoreType.DMA((rows // row_block,)),
        ],
        compiler_params=pltpu.CompilerParams(
            dimension_semantics=("arbitrary",), vmem_limit_bytes=60 * 1024 * 1024
        ),
        cost_estimate=pl.CostEstimate(
            flops=2 * rows * vocab * width,
            transcendentals=rows * vocab,
            bytes_accessed=rows * width * 4 + vocab * width * 2 + rows * 20,
        ),
    )(states, norm_gain[None, :], embedding, in_shard_id[None, :])
    return outs


def body(final_states, norm_gain, embedding, targets, deal):
    owners = lax.axis_size("req")
    own_rows = final_states.shape[0]
    shard_cols = embedding.shape[0]
    member = (jnp.arange(owners, dtype=jnp.int32)[:, None] == (deal // own_rows)[None, :])
    counts = lax.all_gather(jnp.sum(member.astype(jnp.int32), axis=1), "req")
    live_count = jnp.sum(counts[:, lax.axis_index("req")])
    live = jnp.arange(own_rows, dtype=jnp.int32) < live_count

    stats = shard_stats(final_states, norm_gain, embedding, targets)
    group = lax.axis_size("tp")
    pieces = [stats]
    for shift in range(1, group):
        pieces.append(
            lax.ppermute(stats, "tp", [(d, (d + shift) % group) for d in range(group)])
        )
    gathered = jnp.stack(pieces)
    peaks = gathered[:, 0]
    row_peak = jnp.max(peaks, axis=0)
    scale = jnp.exp(peaks - row_peak[None, :])
    exp_total = jnp.sum(gathered[:, 1] * scale, axis=0)
    moment = jnp.sum(gathered[:, 2] * scale, axis=0)
    chosen = jnp.sum(gathered[:, 3], axis=0)
    log_total = row_peak + jnp.log(exp_total)
    expected = moment / exp_total
    logprob = jnp.where(live, chosen - log_total, 0.0)
    entropy = jnp.where(live, log_total - expected, 0.0)
    return (logprob, entropy)


def solution(mesh):
    return jax.shard_map(
        body,
        mesh=mesh,
        in_specs=(P("req", None), P(), P("tp", None), P("req"), P("req")),
        out_specs=(P("req"), P("req")),
        check_vma=False,
    )
```

```python
import functools

import jax
import jax.numpy as jnp
from jax import lax
from jax.experimental import pallas as pl
from jax.experimental.pallas import tpu as pltpu
from jax.sharding import PartitionSpec as P


def rms_normed(states, norm_gain):
    mean_square = jnp.mean(states * states, axis=1, keepdims=True)
    return (states * lax.rsqrt(mean_square + 1e-06) * norm_gain[None, :]).astype(jnp.bfloat16)


def shard_stats_xla(normed, embedding, in_shard_id):
    logits = lax.dot_general(
        normed, embedding, (((1,), (1,)), ((), ())), preferred_element_type=jnp.float32
    )
    peak = jnp.max(logits, axis=1)
    weights = jnp.exp(logits - peak[:, None])
    total = jnp.sum(weights, axis=1)
    moment = jnp.sum(weights * logits, axis=1)
    cols = lax.broadcasted_iota(jnp.int32, logits.shape, 1)
    chosen = jnp.sum(jnp.where(cols == in_shard_id[:, None], logits, 0.0), axis=1)
    return jnp.stack((peak, total, moment, chosen))


LIFT = 40.0
SAFE = 60.0


def stats_kernel(row_block, states_ref, gain_ref, emb_ref, ids_ref, stats_ref, normed_ref, saved_ref):
    j = pl.program_id(0)
    col_block = emb_ref.shape[0]
    vocab_ids = lax.broadcasted_iota(jnp.int32, (col_block, row_block), 0)
    peak_ref, total_ref, moment_ref, chosen_ref = (stats_ref.at[k:k + 1] for k in range(4))

    @pl.when(j == 0)
    def _():
        for r in range(normed_ref.shape[0] // row_block):
            rows = pl.ds(r * row_block, row_block)
            x = states_ref[rows, :]
            mean_square = jnp.mean(x * x, axis=1, keepdims=True)
            normed_ref[rows, :] = (x * lax.rsqrt(mean_square + 1e-06) * gain_ref[...]).astype(jnp.bfloat16)
        peak_ref[...] = jnp.full(peak_ref.shape, -1e30, jnp.float32)
        total_ref[...] = jnp.zeros(total_ref.shape, jnp.float32)
        moment_ref[...] = jnp.zeros(moment_ref.shape, jnp.float32)
        chosen_ref[...] = jnp.zeros(chosen_ref.shape, jnp.float32)

    def logits_of(rows):
        return lax.dot_general(
            emb_ref[...], normed_ref[rows, :], (((1,), (1,)), ((), ())),
            preferred_element_type=jnp.float32,
        )

    def add_chosen(rows, logits):
        local_id = ids_ref[:, rows] - (lax.axis_index("tp") * pl.num_programs(0) + j) * col_block
        chosen_ref[:, rows] = chosen_ref[:, rows] + jnp.sum(
            jnp.where(vocab_ids == local_id, logits, 0.0), axis=0, keepdims=True
        )

    def rows_of(r):
        return pl.ds(pl.multiple_of(r * row_block, row_block), row_block)

    def exact_chunk(r, carry):
        rows = rows_of(r)
        logits = logits_of(rows)
        old_peak = peak_ref[:, rows]
        new_peak = jnp.maximum(old_peak, jnp.max(logits, axis=0, keepdims=True))
        weights = jnp.exp(logits - new_peak)
        scale = jnp.exp(old_peak - new_peak)
        total_ref[:, rows] = total_ref[:, rows] * scale + jnp.sum(weights, axis=0, keepdims=True)
        moment_ref[:, rows] = moment_ref[:, rows] * scale + jnp.sum(weights * logits, axis=0, keepdims=True)
        peak_ref[:, rows] = new_peak
        add_chosen(rows, logits)
        return carry

    def fast_chunk(r, worst):
        rows = rows_of(r)
        logits = logits_of(rows)
        old_peak = peak_ref[:, rows]
        shift = old_peak + LIFT
        tile_peak = jnp.max(logits, axis=0, keepdims=True)
        weights = jnp.exp(logits - shift)
        new_peak = jnp.maximum(old_peak, tile_peak)
        scale = jnp.exp(old_peak - new_peak)
        part_scale = jnp.exp(shift - new_peak)
        total_ref[:, rows] = total_ref[:, rows] * scale + jnp.sum(weights, axis=0, keepdims=True) * part_scale
        moment_ref[:, rows] = moment_ref[:, rows] * scale + jnp.sum(weights * logits, axis=0, keepdims=True) * part_scale
        peak_ref[:, rows] = new_peak
        add_chosen(rows, logits)
        return jnp.maximum(worst, tile_peak - old_peak)

    n_chunks = normed_ref.shape[0] // row_block

    @pl.when(j == 0)
    def _():
        lax.fori_loop(0, n_chunks, exact_chunk, 0, unroll=True)

    @pl.when(j > 0)
    def _():
        saved_ref[...] = stats_ref[...]
        worst = lax.fori_loop(
            0, n_chunks, fast_chunk, jnp.full((1, row_block), -1e30, jnp.float32), unroll=True
        )

        @pl.when(jnp.max(worst) > SAFE)
        def _():
            stats_ref[...] = saved_ref[...]
            lax.fori_loop(0, n_chunks, exact_chunk, 0, unroll=True)


def shard_stats(states, norm_gain, embedding, in_shard_id, col_block=1024, row_block=256):
    rows, width = states.shape
    vocab = embedding.shape[0]
    col_block = min(col_block, vocab)
    row_block = min(row_block, rows)
    stat = jax.ShapeDtypeStruct((4, rows), jnp.float32)
    resident = pl.BlockSpec((4, rows), lambda j: (0, 0))
    outs = pl.pallas_call(
        functools.partial(stats_kernel, row_block),
        grid=(vocab // col_block,),
        in_specs=[
            pl.BlockSpec((rows, width), lambda j: (0, 0)),
            pl.BlockSpec((1, width), lambda j: (0, 0)),
            pl.BlockSpec((col_block, width), lambda j: (j, 0)),
            pl.BlockSpec((1, rows), lambda j: (0, 0)),
        ],
        out_specs=resident,
        out_shape=stat,
        scratch_shapes=[pltpu.VMEM((rows, width), jnp.bfloat16), pltpu.VMEM((4, rows), jnp.float32)],
        compiler_params=pltpu.CompilerParams(
            dimension_semantics=("arbitrary",), vmem_limit_bytes=60 * 1024 * 1024
        ),
        cost_estimate=pl.CostEstimate(
            flops=2 * rows * vocab * width,
            transcendentals=rows * vocab,
            bytes_accessed=rows * width * 4 + vocab * width * 2 + rows * 20,
        ),
    )(states, norm_gain[None, :], embedding, in_shard_id[None, :])
    return outs


def body(final_states, norm_gain, embedding, targets, deal):
    owners = lax.axis_size("req")
    own_rows = final_states.shape[0]
    shard_cols = embedding.shape[0]
    member = (jnp.arange(owners, dtype=jnp.int32)[:, None] == (deal // own_rows)[None, :])
    counts = lax.all_gather(jnp.sum(member.astype(jnp.int32), axis=1), "req")
    live_count = jnp.sum(counts[:, lax.axis_index("req")])
    live = jnp.arange(own_rows, dtype=jnp.int32) < live_count

    stats = shard_stats(final_states, norm_gain, embedding, targets)
    group = lax.axis_size("tp")
    pieces = [stats]
    for shift in range(1, group):
        pieces.append(
            lax.ppermute(stats, "tp", [(d, (d + shift) % group) for d in range(group)])
        )
    row_peak = functools.reduce(jnp.maximum, [piece[0] for piece in pieces])
    scales = [jnp.exp(piece[0] - row_peak) for piece in pieces]
    exp_total = sum(piece[1] * s for piece, s in zip(pieces, scales))
    moment = sum(piece[2] * s for piece, s in zip(pieces, scales))
    chosen = sum(piece[3] for piece in pieces)
    log_total = row_peak + jnp.log(exp_total)
    expected = moment / exp_total
    logprob = jnp.where(live, chosen - log_total, 0.0)
    entropy = jnp.where(live, log_total - expected, 0.0)
    return (logprob, entropy)


def solution(mesh):
    return jax.shard_map(
        body,
        mesh=mesh,
        in_specs=(P("req", None), P(), P("tp", None), P("req"), P("req")),
        out_specs=(P("req"), P("req")),
        check_vma=False,
    )
```

```python
import functools

import jax
import jax.numpy as jnp
from jax import lax
from jax.experimental import pallas as pl
from jax.experimental.pallas import tpu as pltpu
from jax.sharding import PartitionSpec as P


def rms_normed(states, norm_gain):
    mean_square = jnp.mean(states * states, axis=1, keepdims=True)
    return (states * lax.rsqrt(mean_square + 1e-06) * norm_gain[None, :]).astype(jnp.bfloat16)


def shard_stats_xla(normed, embedding, in_shard_id):
    logits = lax.dot_general(
        normed, embedding, (((1,), (1,)), ((), ())), preferred_element_type=jnp.float32
    )
    peak = jnp.max(logits, axis=1)
    weights = jnp.exp(logits - peak[:, None])
    total = jnp.sum(weights, axis=1)
    moment = jnp.sum(weights * logits, axis=1)
    cols = lax.broadcasted_iota(jnp.int32, logits.shape, 1)
    chosen = jnp.sum(jnp.where(cols == in_shard_id[:, None], logits, 0.0), axis=1)
    return jnp.stack((peak, total, moment, chosen))


LIFT = 40.0
SAFE = 60.0


def stats_kernel(row_block, states_ref, gain_ref, emb_ref, ids_ref, stats_ref, normed_ref, saved_ref):
    j = pl.program_id(0)
    col_block = emb_ref.shape[0]
    vocab_ids = lax.broadcasted_iota(jnp.int32, (col_block, row_block), 0)
    peak_ref, total_ref, moment_ref, chosen_ref = (stats_ref.at[k:k + 1] for k in range(4))

    @pl.when(j == 0)
    def _():
        for r in range(normed_ref.shape[0] // row_block):
            rows = pl.ds(r * row_block, row_block)
            x = states_ref[rows, :]
            mean_square = jnp.mean(x * x, axis=1, keepdims=True)
            normed_ref[rows, :] = (x * lax.rsqrt(mean_square + 1e-06) * gain_ref[...]).astype(jnp.bfloat16)
        peak_ref[...] = jnp.full(peak_ref.shape, -1e30, jnp.float32)
        total_ref[...] = jnp.zeros(total_ref.shape, jnp.float32)
        moment_ref[...] = jnp.zeros(moment_ref.shape, jnp.float32)
        chosen_ref[...] = jnp.zeros(chosen_ref.shape, jnp.float32)

    def logits_of(rows):
        return lax.dot_general(
            emb_ref[...], normed_ref[rows, :], (((1,), (1,)), ((), ())),
            preferred_element_type=jnp.float32,
        )

    def add_chosen(rows, logits):
        local_id = ids_ref[:, rows] - (lax.axis_index("tp") * pl.num_programs(0) + j) * col_block
        chosen_ref[:, rows] = chosen_ref[:, rows] + jnp.sum(
            jnp.where(vocab_ids == local_id, logits, 0.0), axis=0, keepdims=True
        )

    def rows_of(r):
        return pl.ds(pl.multiple_of(r * row_block, row_block), row_block)

    def exact_chunk(r, carry):
        rows = rows_of(r)
        logits = logits_of(rows)
        old_peak = peak_ref[:, rows]
        new_peak = jnp.maximum(old_peak, jnp.max(logits, axis=0, keepdims=True))
        weights = jnp.exp(logits - new_peak)
        scale = jnp.exp(old_peak - new_peak)
        total_ref[:, rows] = total_ref[:, rows] * scale + jnp.sum(weights, axis=0, keepdims=True)
        moment_ref[:, rows] = moment_ref[:, rows] * scale + jnp.sum(weights * logits, axis=0, keepdims=True)
        peak_ref[:, rows] = new_peak
        add_chosen(rows, logits)
        return carry

    def fast_chunk(r, worst):
        rows = rows_of(r)
        logits = logits_of(rows)
        old_peak = peak_ref[:, rows]
        shift = old_peak + LIFT
        tile_peak = jnp.max(logits, axis=0, keepdims=True)
        weights = jnp.exp(logits - shift)
        new_peak = jnp.maximum(old_peak, tile_peak)
        scale = jnp.exp(old_peak - new_peak)
        part_scale = jnp.exp(shift - new_peak)
        total_ref[:, rows] = total_ref[:, rows] * scale + jnp.sum(weights, axis=0, keepdims=True) * part_scale
        moment_ref[:, rows] = moment_ref[:, rows] * scale + jnp.sum(weights * logits, axis=0, keepdims=True) * part_scale
        peak_ref[:, rows] = new_peak
        add_chosen(rows, logits)
        return jnp.maximum(worst, tile_peak - old_peak)

    n_chunks = normed_ref.shape[0] // row_block

    @pl.when(j == 0)
    def _():
        lax.fori_loop(0, n_chunks, exact_chunk, 0, unroll=True)

    @pl.when(j > 0)
    def _():
        saved_ref[...] = stats_ref[...]
        worst = lax.fori_loop(
            0, n_chunks, fast_chunk, jnp.full((1, row_block), -1e30, jnp.float32), unroll=True
        )

        @pl.when(jnp.max(worst) > SAFE)
        def _():
            stats_ref[...] = saved_ref[...]
            lax.fori_loop(0, n_chunks, exact_chunk, 0, unroll=True)


def shard_stats(states, norm_gain, embedding, in_shard_id, col_block=1024, row_block=256):
    rows, width = states.shape
    vocab = embedding.shape[0]
    col_block = min(col_block, vocab)
    row_block = min(row_block, rows)
    stat = jax.ShapeDtypeStruct((4, rows), jnp.float32)
    resident = pl.BlockSpec((4, rows), lambda j: (0, 0))
    outs = pl.pallas_call(
        functools.partial(stats_kernel, row_block),
        grid=(vocab // col_block,),
        in_specs=[
            pl.BlockSpec((rows, width), lambda j: (0, 0)),
            pl.BlockSpec((1, width), lambda j: (0, 0)),
            pl.BlockSpec((col_block, width), lambda j: (j, 0)),
            pl.BlockSpec((1, rows), lambda j: (0, 0)),
        ],
        out_specs=resident,
        out_shape=stat,
        scratch_shapes=[pltpu.VMEM((rows, width), jnp.bfloat16), pltpu.VMEM((4, rows), jnp.float32)],
        compiler_params=pltpu.CompilerParams(
            dimension_semantics=("arbitrary",), vmem_limit_bytes=60 * 1024 * 1024
        ),
        cost_estimate=pl.CostEstimate(
            flops=2 * rows * vocab * width,
            transcendentals=rows * vocab,
            bytes_accessed=rows * width * 4 + vocab * width * 2 + rows * 20,
        ),
    )(states, norm_gain[None, :], embedding, in_shard_id[None, :])
    return outs


def body(final_states, norm_gain, embedding, targets, deal):
    owners = lax.axis_size("req")
    own_rows = final_states.shape[0]
    shard_cols = embedding.shape[0]
    member = (jnp.arange(owners, dtype=jnp.int32)[:, None] == (deal // own_rows)[None, :])
    counts = lax.all_gather(jnp.sum(member.astype(jnp.int32), axis=1), "req")
    live_count = jnp.sum(counts[:, lax.axis_index("req")])
    live = jnp.arange(own_rows, dtype=jnp.int32) < live_count

    stats = shard_stats(final_states, norm_gain, embedding, targets)
    group = lax.axis_size("tp")
    pieces = [stats]
    for shift in range(1, group):
        pieces.append(
            lax.ppermute(stats, "tp", [(d, (d + shift) % group) for d in range(group)])
        )
    row_peak = functools.reduce(jnp.maximum, [piece[0] for piece in pieces])
    scales = [jnp.exp(piece[0] - row_peak) for piece in pieces]
    def same_on_every_copy(terms):
        if len(terms) == 4:
            return (terms[0] + terms[2]) + (terms[1] + terms[3])
        return sum(terms)

    exp_total = same_on_every_copy([piece[1] * s for piece, s in zip(pieces, scales)])
    moment = same_on_every_copy([piece[2] * s for piece, s in zip(pieces, scales)])
    chosen = same_on_every_copy([piece[3] for piece in pieces])
    log_total = row_peak + jnp.log(exp_total)
    expected = moment / exp_total
    logprob = jnp.where(live, chosen - log_total, 0.0)
    entropy = jnp.where(live, log_total - expected, 0.0)
    return (logprob, entropy)


def solution(mesh):
    return jax.shard_map(
        body,
        mesh=mesh,
        in_specs=(P("req", None), P(), P("tp", None), P("req"), P("req")),
        out_specs=(P("req"), P("req")),
        check_vma=False,
    )
```
